128 devices in a mesh: dp: 8 (over x_lo, z), wshard: 4 (over y), tensor: 4 (over x_hi, core).
Axes of the slice: x: 4 (x_hi: 2, x_lo: 2; x = x_hi * 2 + x_lo), y: 4, z: 4, core: 2. Of those that a mesh axis runs over, the one named last changes fastest.
Arguments:
- expert_grads: bfloat16 [8, 4, 768, 2048], P('dp', 'wshard', None, 'tensor'), may hold values from -6 to 6
- dense_grads: bfloat16 [8, 768, 2048], P('dp', 'wshard', 'tensor'), may hold values from -6 to 6
- expert_master: float32 [4, 768, 2048], P('wshard', None, ('tensor', 'dp')), may hold values from -0.6 to 0.6
- expert_first: float32 [4, 768, 2048], P('wshard', None, ('tensor', 'dp')), may hold values from -3 to 3
- expert_second: float32 [4, 768, 2048], P('wshard', None, ('tensor', 'dp')), may hold values from 0.01 to 1
- expert_stat: float32 [4, 768, 768], P('wshard', ('tensor', 'dp')), as said below
- expert_basis: float32 [4, 768, 768], P('wshard'), may hold values from -0.21875 to 0.21875
- dense_master: float32 [768, 2048], P('wshard', ('tensor', 'dp')), may hold values from -0.6 to 0.6
- dense_first: float32 [768, 2048], P('wshard', ('tensor', 'dp')), may hold values from -3 to 3
- dense_second: float32 [768, 2048], P(None, ('tensor', 'dp')), may hold values from 0.01 to 1
- dense_stat: float32 [768, 768], P(('tensor', 'dp')), as said below
- dense_basis: float32 [768, 768], replicated, may hold values from -0.21875 to 0.21875
Outputs:
- expert_master_out: float32 [4, 768, 2048], P('wshard', None, ('tensor', 'dp'))
- expert_first_out: float32 [4, 768, 2048], P('wshard', None, ('tensor', 'dp'))
- expert_second_out: float32 [4, 768, 2048], P('wshard', None, ('tensor', 'dp'))
- expert_stat_out: float32 [4, 768, 768], P('wshard', ('tensor', 'dp'))
- expert_basis_out: float32 [4, 768, 768], P('wshard')
- expert_weights: bfloat16 [4, 768, 2048], P('wshard', None, 'tensor')
- dense_master_out: float32 [768, 2048], P('wshard', ('tensor', 'dp'))
- dense_first_out: float32 [768, 2048], P('wshard', ('tensor', 'dp'))
- dense_second_out: float32 [768, 2048], P(None, ('tensor', 'dp'))
- dense_stat_out: float32 [768, 768], P(('tensor', 'dp'))
- dense_basis_out: float32 [768, 768], replicated
- dense_weights: bfloat16 [768, 2048], P('wshard', 'tensor')
The draws below stay inside these ranges and needn't reach their ends.
Inputs may be any that keep to these rules, and one draw needn't show every extreme that they name: `expert_stat`: symmetric running statistics of each expert. `dense_stat`: A symmetric running statistic.
All inputs are finite; a program needn't handle non-finite values.
Results may differ from the reference program's by a relative error of at most 0.001.
Values may be sent and summed in bfloat16 or wider, within the bound.
No kernel may reach another device: no remote copies, remote signals or barrier semaphores. Data moves between devices by JAX's collectives and lax.ppermute only.
A program may use at most 128 MiB of HBM per device.

```python
import math
import jax
import jax.numpy as jnp
from jax import lax

D = 768
FF = 2048
NS_ITERS = 3
EXPERTS = 4
N_DP = 8


def symmetric_stat(key, leading):
    shape = leading + (D, D)
    key_off = jax.random.fold_in(key, 11)
    key_diag = jax.random.fold_in(key, 12)
    raw = jax.random.normal(key_off, shape, jnp.float32) * 0.035
    log_diag = jax.random.uniform(key_diag, leading + (D,), jnp.float32, 0.0, jnp.log(10.0))
    sym_part = raw + jnp.swapaxes(raw, -1, -2)
    rows_index = lax.broadcasted_iota(jnp.int32, (D, D), 0)
    cols_index = lax.broadcasted_iota(jnp.int32, (D, D), 1)
    identity = (rows_index == cols_index).astype(jnp.float32)
    return sym_part + identity * jnp.exp(log_diag)[..., None]


def draw_expert_stat(key, part):
    return symmetric_stat(key, (EXPERTS,))


def draw_dense_stat(key, part):
    return symmetric_stat(key, ())


def with_spikes(drawn, key, source, target, parts, factor):
    owner, partner = [(jnp.arange(drawn.shape[position]) // (drawn.shape[position] // parts)).reshape([-1 if axis == position else 1 for axis in range(drawn.ndim)]) for position in (source, target)]
    chosen = jax.random.permutation(key, parts)[partner]
    strong = (owner == chosen) | (owner == (partner + parts // 2) % parts)
    return jnp.where(strong, factor * drawn, drawn)


def level_of(own_key, shape, shards, smallest, largest):
    factor_of, own = 1.0, jax.random.fold_in(own_key, 6)
    for dim, shards_of in shards:
        steps = jnp.exp(jax.random.uniform(jax.random.fold_in(own, dim), (shards_of,), jnp.float32, smallest / len(shards), largest / len(shards)))
        factor_of = factor_of * jnp.repeat(steps, shape[dim] // shards_of).reshape([-1 if axis == dim else 1 for axis in range(len(shape))])
    return factor_of


def bell_draw(own_key, extent, spread, limit, shards=(), dtype=jnp.bfloat16):
    level = level_of(own_key, extent, shards, -0.22, 0.18) if shards else 1.0
    drawn = jax.random.normal(own_key, extent, jnp.float32) * spread * level
    return jnp.minimum(jnp.maximum(drawn, -limit), limit).astype(dtype)


def gaussian_with(rng, extent, spread, bound, cuts, heavy, dtype=jnp.bfloat16):
    values = spread * jax.random.normal(rng, extent, jnp.float32)
    if cuts:
        values = values * level_of(rng, extent, cuts, -0.22, 0.18)
    return jnp.clip(with_spikes(values, jax.random.fold_in(rng, 3), *heavy), -bound, bound).astype(dtype)


def setup_inputs(seed: int = 0) -> dict:
    seeds = jax.random.split(jax.random.key(seed), 13)
    return {
        "expert_grads": gaussian_with(seeds[0], (N_DP, EXPERTS, D, FF), 1.0, 6.0, ((0, 8), (1, 4), (3, 4)), (0, 3, 8, 2.0)),
        "dense_grads": gaussian_with(seeds[1], (N_DP, D, FF), 1.0, 6.0, ((0, 8), (1, 4), (2, 4)), (0, 2, 8, 2.0)),
        "expert_master": bell_draw(seeds[2], (EXPERTS, D, FF), 0.1, 0.6, ((0, 4), (2, 32)), jnp.float32),
        "expert_first": bell_draw(seeds[3], (EXPERTS, D, FF), 0.5, 3.0, ((0, 4), (2, 32)), jnp.float32),
        "expert_second": jnp.clip(jnp.exp(math.log(1.0) - 4.6051702 * jax.random.uniform(seeds[4], (EXPERTS, D, FF), jnp.float32) ** level_of(seeds[4], (EXPERTS, D, FF), ((0, 4), (2, 32)), -0.2, 0.2)), 0.01, 1.0),
        "expert_stat": draw_expert_stat(jax.random.fold_in(seeds[12], 71), 0),
        "expert_basis": bell_draw(seeds[6], (EXPERTS, D, D), D ** -0.5, 0.21875, ((0, 4),), jnp.float32),
        "dense_master": bell_draw(seeds[7], (D, FF), 0.1, 0.6, ((0, 4), (1, 32)), jnp.float32),
        "dense_first": bell_draw(seeds[8], (D, FF), 0.5, 3.0, ((0, 4), (1, 32)), jnp.float32),
        "dense_second": jnp.clip(jnp.exp(math.log(1.0) - 4.6051702 * jax.random.uniform(seeds[9], (D, FF), jnp.float32) ** level_of(seeds[9], (D, FF), ((1, 32),), -0.2, 0.2)), 0.01, 1.0),
        "dense_stat": draw_dense_stat(jax.random.fold_in(seeds[12], 71), 0),
        "dense_basis": bell_draw(seeds[11], (D, D), D ** -0.5, 0.21875, (), jnp.float32),
    }


HIGHEST = lax.Precision.HIGHEST
linear_coef = 3.4445
cubic_coef = -4.775
quintic_coef = 2.0315

def orthogonalize(power):
    square_sum = jnp.sum(power * power)
    current = power * lax.rsqrt(square_sum + 1e-06)
    for repeat in range(NS_ITERS):
        gram_matrix = jnp.matmul(current.T, current, precision=HIGHEST)
        first_prod = jnp.matmul(current, gram_matrix, precision=HIGHEST)
        second_prod = jnp.matmul(first_prod, gram_matrix, precision=HIGHEST)
        current = linear_coef * current + cubic_coef * first_prod + quintic_coef * second_prod
    return current

def soap_matrix(grad_mean, master, first, second, stat, basis):
    first_out = 0.9 * first + 0.1 * grad_mean
    rotated = jnp.matmul(basis.T, jnp.concatenate([grad_mean, first_out], 1), precision=HIGHEST)
    grad_rot = rotated[:, :FF]
    first_rot = rotated[:, FF:]
    second_out = 0.95 * second + 0.05 * grad_rot * grad_rot
    scaled = first_rot / (jnp.sqrt(second_out) + 1e-08)
    update = jnp.matmul(basis, scaled, precision=HIGHEST)
    master_out = master - 0.05 * update
    stat_out = 0.95 * stat + 0.05 * jnp.matmul(grad_mean, grad_mean.T, precision=HIGHEST)
    power = jnp.matmul(stat_out, basis, precision=HIGHEST)
    basis_out = orthogonalize(power)
    return (master_out, first_out, second_out, stat_out, basis_out, master_out.astype(jnp.bfloat16))

def reference(expert_grads, dense_grads, expert_master, expert_first, expert_second, expert_stat, expert_basis, dense_master, dense_first, dense_second, dense_stat, dense_basis):
    expert_mean = lax.optimization_barrier(jnp.sum(expert_grads.astype(jnp.float32), 0)) / N_DP
    dense_mean = lax.optimization_barrier(jnp.sum(dense_grads.astype(jnp.float32), 0)) / N_DP
    results = []
    for expert in range(EXPERTS):
        results.append(soap_matrix(expert_mean[expert], expert_master[expert], expert_first[expert], expert_second[expert], expert_stat[expert], expert_basis[expert]))
    stacked = [jnp.stack([item[index] for item in results], 0) for index in range(6)]
    dense_out = soap_matrix(dense_mean, dense_master, dense_first, dense_second, dense_stat, dense_basis)
    return (stacked[0], stacked[1], stacked[2], stacked[3], stacked[4], stacked[5], dense_out[0], dense_out[1], dense_out[2], dense_out[3], dense_out[4], dense_out[5])
```

```python
import jax
import jax.numpy as jnp
from jax import lax
from jax.sharding import PartitionSpec as P

NS_ITERS = 3


HIGHEST = lax.Precision.HIGHEST
linear_coef = 3.4445
cubic_coef = -4.775
quintic_coef = 2.0315


def local_gram(current):
    return jnp.einsum("bki,bkj->bij", current, current, precision=HIGHEST)


def quintic_step(current, gram_matrix):
    first_prod = jnp.einsum("bik,bkj->bij", current, gram_matrix, precision=HIGHEST)
    second_prod = jnp.einsum("bik,bkj->bij", first_prod, gram_matrix, precision=HIGHEST)
    return linear_coef * current + cubic_coef * first_prod + quintic_coef * second_prod


def shards(
    expert_grads,
    dense_grads,
    expert_master,
    expert_first,
    expert_second,
    expert_stat,
    expert_basis,
    dense_master,
    dense_first,
    dense_second,
    dense_stat,
    dense_basis,
):
    replicas = lax.axis_size("dp")
    experts_here = expert_grads.shape[1]
    expert_local = expert_grads.reshape(expert_grads.shape[1:]).astype(jnp.float32)
    dense_local = dense_grads.reshape(dense_grads.shape[1:]).astype(jnp.float32)
    expert_sum, dense_sum = (
        lax.psum_scatter(expert_local, "dp", scatter_dimension=2, tiled=True),
        lax.psum_scatter(dense_local, "dp", scatter_dimension=1, tiled=True),
    )
    expert_mean = expert_sum / replicas
    dense_mean = dense_sum / replicas
    expert_first_out = 0.9 * expert_first + 0.1 * expert_mean
    dense_first_out = 0.9 * dense_first + 0.1 * dense_mean
    dense_grad_full, dense_first_full = (
        lax.all_gather(dense_mean, "wshard", axis=0, tiled=True),
        lax.all_gather(dense_first_out, "wshard", axis=0, tiled=True),
    )
    grads_all = jnp.concatenate([expert_mean, dense_grad_full[None]], 0)
    firsts_all = jnp.concatenate([expert_first_out, dense_first_full[None]], 0)
    bases_all = jnp.concatenate([expert_basis, dense_basis[None]], 0)
    seconds_all = jnp.concatenate([expert_second, dense_second[None]], 0)
    columns = grads_all.shape[2]
    rotated = jnp.einsum(
        "bki,bkc->bic", bases_all, jnp.concatenate([grads_all, firsts_all], 2), precision=HIGHEST
    )
    grad_rot = rotated[:, :, :columns]
    first_rot = rotated[:, :, columns:]
    seconds_out = 0.95 * seconds_all + 0.05 * grad_rot * grad_rot
    scaled = first_rot / (jnp.sqrt(seconds_out) + 1e-08)
    update = jnp.einsum("bik,bkc->bic", bases_all, scaled, precision=HIGHEST)
    expert_master_out = expert_master - 0.05 * update[:experts_here]
    dense_rows_here = dense_master.shape[0]
    dense_update = lax.dynamic_slice_in_dim(
        update[experts_here], lax.axis_index("wshard") * dense_rows_here, dense_rows_here, 0
    )
    dense_master_out = dense_master - 0.05 * dense_update
    expert_weights, dense_weights = (
        lax.all_gather(expert_master_out.astype(jnp.bfloat16), "dp", axis=2, tiled=True),
        lax.all_gather(dense_master_out.astype(jnp.bfloat16), "dp", axis=1, tiled=True),
    )
    partial_stat = jnp.einsum("bic,bjc->bji", grads_all, grads_all, precision=HIGHEST)
    summed = lax.psum_scatter(partial_stat, ("tensor", "dp"), scatter_dimension=2, tiled=True)
    stats_all = jnp.concatenate([expert_stat, dense_stat[None]], 0)
    stats_out = 0.95 * stats_all + 0.05 * jnp.transpose(summed, (0, 2, 1))
    power_rows = jnp.einsum("bik,bkj->bij", stats_out, bases_all, precision=HIGHEST)
    power = lax.all_gather(power_rows, ("tensor", "dp"), axis=1, tiled=True)
    square_sum = jnp.sum(power * power, (1, 2))
    current = power * lax.rsqrt(square_sum + 1e-06)[:, None, None]
    def ns_iteration(repeat, current):
        return quintic_step(current, local_gram(current))

    current = lax.fori_loop(0, NS_ITERS, ns_iteration, current)
    bases_out = current
    return (
        expert_master_out,
        expert_first_out,
        seconds_out[:experts_here],
        stats_out[:experts_here],
        bases_out[:experts_here],
        expert_weights,
        dense_master_out,
        dense_first_out,
        seconds_out[experts_here],
        stats_out[experts_here],
        bases_out[experts_here],
        dense_weights,
    )


def solution(mesh):
    in_specs = (
        P("dp", "wshard", None, "tensor"),
        P("dp", "wshard", "tensor"),
        P("wshard", None, ("tensor", "dp")),
        P("wshard", None, ("tensor", "dp")),
        P("wshard", None, ("tensor", "dp")),
        P("wshard", ("tensor", "dp"), None),
        P("wshard", None, None),
        P("wshard", ("tensor", "dp")),
        P("wshard", ("tensor", "dp")),
        P(None, ("tensor", "dp")),
        P(("tensor", "dp"), None),
        P(),
    )
    out_specs = (
        P("wshard", None, ("tensor", "dp")),
        P("wshard", None, ("tensor", "dp")),
        P("wshard", None, ("tensor", "dp")),
        P("wshard", ("tensor", "dp"), None),
        P("wshard", None, None),
        P("wshard", None, "tensor"),
        P("wshard", ("tensor", "dp")),
        P("wshard", ("tensor", "dp")),
        P(None, ("tensor", "dp")),
        P(("tensor", "dp"), None),
        P(),
        P("wshard", "tensor"),
    )
    return jax.shard_map(shards, mesh=mesh, in_specs=in_specs, out_specs=out_specs, check_vma=False)
```

```python
import jax
import jax.numpy as jnp
from jax import lax
from jax.sharding import PartitionSpec as P

NS_ITERS = 3


HIGHEST = lax.Precision.HIGHEST
HIGH = lax.Precision.HIGH
linear_coef = 3.4445
cubic_coef = -4.775
quintic_coef = 2.0315


def local_gram(current):
    return jnp.einsum("bki,bkj->bij", current, current, precision=HIGH)


def quintic_step(current, gram_matrix):
    first_prod = jnp.einsum("bik,bkj->bij", current, gram_matrix, precision=HIGH)
    second_prod = jnp.einsum("bik,bkj->bij", first_prod, gram_matrix, precision=HIGH)
    return linear_coef * current + cubic_coef * first_prod + quintic_coef * second_prod


def shards(
    expert_grads,
    dense_grads,
    expert_master,
    expert_first,
    expert_second,
    expert_stat,
    expert_basis,
    dense_master,
    dense_first,
    dense_second,
    dense_stat,
    dense_basis,
):
    replicas = lax.axis_size("dp")
    experts_here = expert_grads.shape[1]
    expert_local = expert_grads.reshape(expert_grads.shape[1:]).astype(jnp.float32)
    dense_local = dense_grads.reshape(dense_grads.shape[1:]).astype(jnp.float32)
    expert_sum, dense_sum = (
        lax.psum_scatter(expert_local, "dp", scatter_dimension=2, tiled=True),
        lax.psum_scatter(dense_local, "dp", scatter_dimension=1, tiled=True),
    )
    expert_mean = expert_sum / replicas
    dense_mean = dense_sum / replicas
    expert_first_out = 0.9 * expert_first + 0.1 * expert_mean
    dense_first_out = 0.9 * dense_first + 0.1 * dense_mean
    dense_grad_full, dense_first_full = (
        lax.all_gather(dense_mean, "wshard", axis=0, tiled=True),
        lax.all_gather(dense_first_out, "wshard", axis=0, tiled=True),
    )
    grads_all = jnp.concatenate([expert_mean, dense_grad_full[None]], 0)
    firsts_all = jnp.concatenate([expert_first_out, dense_first_full[None]], 0)
    bases_all = jnp.concatenate([expert_basis, dense_basis[None]], 0)
    seconds_all = jnp.concatenate([expert_second, dense_second[None]], 0)
    columns = grads_all.shape[2]
    rotated = jnp.einsum(
        "bki,bkc->bic", bases_all, jnp.concatenate([grads_all, firsts_all], 2), precision=HIGHEST
    )
    grad_rot = rotated[:, :, :columns]
    first_rot = rotated[:, :, columns:]
    seconds_out = 0.95 * seconds_all + 0.05 * grad_rot * grad_rot
    scaled = first_rot / (jnp.sqrt(seconds_out) + 1e-08)
    update = jnp.einsum("bik,bkc->bic", bases_all, scaled, precision=HIGHEST)
    expert_master_out = expert_master - 0.05 * update[:experts_here]
    dense_rows_here = dense_master.shape[0]
    dense_update = lax.dynamic_slice_in_dim(
        update[experts_here], lax.axis_index("wshard") * dense_rows_here, dense_rows_here, 0
    )
    dense_master_out = dense_master - 0.05 * dense_update
    expert_weights, dense_weights = (
        lax.all_gather(expert_master_out.astype(jnp.bfloat16), "dp", axis=2, tiled=True),
        lax.all_gather(dense_master_out.astype(jnp.bfloat16), "dp", axis=1, tiled=True),
    )
    partial_stat = jnp.einsum("bic,bjc->bji", grads_all, grads_all, precision=HIGHEST)
    summed = lax.psum_scatter(partial_stat, ("tensor", "dp"), scatter_dimension=2, tiled=True)
    stats_all = jnp.concatenate([expert_stat, dense_stat[None]], 0)
    stats_out = 0.95 * stats_all + 0.05 * jnp.transpose(summed, (0, 2, 1))
    power_rows = jnp.einsum("bik,bkj->bij", stats_out, bases_all, precision=HIGH)
    power = lax.all_gather(power_rows, ("tensor", "dp"), axis=1, tiled=True)
    square_sum = jnp.sum(power * power, (1, 2))
    current = power * lax.rsqrt(square_sum + 1e-06)[:, None, None]
    def ns_iteration(repeat, current):
        return quintic_step(current, local_gram(current))

    current = lax.fori_loop(0, NS_ITERS, ns_iteration, current)
    bases_out = current
    return (
        expert_master_out,
        expert_first_out,
        seconds_out[:experts_here],
        stats_out[:experts_here],
        bases_out[:experts_here],
        expert_weights,
        dense_master_out,
        dense_first_out,
        seconds_out[experts_here],
        stats_out[experts_here],
        bases_out[experts_here],
        dense_weights,
    )


def solution(mesh):
    in_specs = (
        P("dp", "wshard", None, "tensor"),
        P("dp", "wshard", "tensor"),
        P("wshard", None, ("tensor", "dp")),
        P("wshard", None, ("tensor", "dp")),
        P("wshard", None, ("tensor", "dp")),
        P("wshard", ("tensor", "dp"), None),
        P("wshard", None, None),
        P("wshard", ("tensor", "dp")),
        P("wshard", ("tensor", "dp")),
        P(None, ("tensor", "dp")),
        P(("tensor", "dp"), None),
        P(),
    )
    out_specs = (
        P("wshard", None, ("tensor", "dp")),
        P("wshard", None, ("tensor", "dp")),
        P("wshard", None, ("tensor", "dp")),
        P("wshard", ("tensor", "dp"), None),
        P("wshard", None, None),
        P("wshard", None, "tensor"),
        P("wshard", ("tensor", "dp")),
        P("wshard", ("tensor", "dp")),
        P(None, ("tensor", "dp")),
        P(("tensor", "dp"), None),
        P(),
        P("wshard", "tensor"),
    )
    return jax.shard_map(shards, mesh=mesh, in_specs=in_specs, out_specs=out_specs, check_vma=False)
```

```python
import jax
import jax.numpy as jnp
from jax import lax
from jax.sharding import PartitionSpec as P

NS_ITERS = 3


HIGHEST = lax.Precision.HIGHEST
HIGH = lax.Precision.HIGH
linear_coef = 3.4445
cubic_coef = -4.775
quintic_coef = 2.0315


def local_gram(current):
    return jnp.einsum("bki,bkj->bij", current, current, precision=HIGH)


def quintic_step(current, gram_matrix):
    first_prod = jnp.einsum("bik,bkj->bij", current, gram_matrix, precision=HIGH)
    second_prod = jnp.einsum("bik,bkj->bij", first_prod, gram_matrix, precision=HIGH)
    return linear_coef * current + cubic_coef * first_prod + quintic_coef * second_prod


def shards(
    expert_grads,
    dense_grads,
    expert_master,
    expert_first,
    expert_second,
    expert_stat,
    expert_basis,
    dense_master,
    dense_first,
    dense_second,
    dense_stat,
    dense_basis,
):
    replicas = lax.axis_size("dp")
    experts_here = expert_grads.shape[1]
    expert_local = expert_grads.reshape(expert_grads.shape[1:]).astype(jnp.float32)
    dense_local = dense_grads.reshape(dense_grads.shape[1:]).astype(jnp.float32)
    expert_sum, dense_sum = (
        lax.psum_scatter(expert_local, "dp", scatter_dimension=2, tiled=True),
        lax.psum_scatter(dense_local, "dp", scatter_dimension=1, tiled=True),
    )
    expert_mean = expert_sum / replicas
    dense_mean = dense_sum / replicas
    expert_first_out = 0.9 * expert_first + 0.1 * expert_mean
    dense_first_out = 0.9 * dense_first + 0.1 * dense_mean
    dense_grad_full, dense_first_full = (
        lax.all_gather(dense_mean, "wshard", axis=0, tiled=True),
        lax.all_gather(dense_first_out, "wshard", axis=0, tiled=True),
    )
    grads_all = jnp.concatenate([expert_mean, dense_grad_full[None]], 0)
    firsts_all = jnp.concatenate([expert_first_out, dense_first_full[None]], 0)
    bases_all = jnp.concatenate([expert_basis, dense_basis[None]], 0)
    seconds_all = jnp.concatenate([expert_second, dense_second[None]], 0)
    columns = grads_all.shape[2]
    rotated = jnp.einsum(
        "bki,bkc->bic", bases_all, jnp.concatenate([grads_all, firsts_all], 2), precision=HIGHEST
    )
    grad_rot = rotated[:, :, :columns]
    first_rot = rotated[:, :, columns:]
    seconds_out = 0.95 * seconds_all + 0.05 * grad_rot * grad_rot
    scaled = first_rot / (jnp.sqrt(seconds_out) + 1e-08)
    update = jnp.einsum("bik,bkc->bic", bases_all, scaled, precision=HIGHEST)
    expert_master_out = expert_master - 0.05 * update[:experts_here]
    dense_rows_here = dense_master.shape[0]
    dense_update = lax.dynamic_slice_in_dim(
        update[experts_here], lax.axis_index("wshard") * dense_rows_here, dense_rows_here, 0
    )
    dense_master_out = dense_master - 0.05 * dense_update
    expert_weights, dense_weights = (
        lax.all_gather(expert_master_out.astype(jnp.bfloat16), "dp", axis=2, tiled=True),
        lax.all_gather(dense_master_out.astype(jnp.bfloat16), "dp", axis=1, tiled=True),
    )
    partial_stat = jnp.einsum("bic,bjc->bij", grads_all, grads_all, precision=HIGHEST)
    stats_all = jnp.concatenate([expert_stat, dense_stat[None]], 0)
    stat_rows = stats_all.shape[1]
    row_start = lax.axis_index(("tensor", "dp")) * stat_rows
    placed = lax.dynamic_update_slice_in_dim(
        jnp.zeros_like(partial_stat), 0.95 * stats_all, row_start, 1
    )
    stats_full = lax.psum(placed + 0.05 * partial_stat, ("tensor", "dp"))
    stats_out = lax.dynamic_slice_in_dim(stats_full, row_start, stat_rows, 1)
    power = jnp.einsum("bik,bkj->bij", stats_full, bases_all, precision=HIGH)
    square_sum = jnp.sum(power * power, (1, 2))
    current = power * lax.rsqrt(square_sum + 1e-06)[:, None, None]
    def ns_iteration(repeat, current):
        return quintic_step(current, local_gram(current))

    current = lax.fori_loop(0, NS_ITERS, ns_iteration, current)
    bases_out = current
    return (
        expert_master_out,
        expert_first_out,
        seconds_out[:experts_here],
        stats_out[:experts_here],
        bases_out[:experts_here],
        expert_weights,
        dense_master_out,
        dense_first_out,
        seconds_out[experts_here],
        stats_out[experts_here],
        bases_out[experts_here],
        dense_weights,
    )


def solution(mesh):
    in_specs = (
        P("dp", "wshard", None, "tensor"),
        P("dp", "wshard", "tensor"),
        P("wshard", None, ("tensor", "dp")),
        P("wshard", None, ("tensor", "dp")),
        P("wshard", None, ("tensor", "dp")),
        P("wshard", ("tensor", "dp"), None),
        P("wshard", None, None),
        P("wshard", ("tensor", "dp")),
        P("wshard", ("tensor", "dp")),
        P(None, ("tensor", "dp")),
        P(("tensor", "dp"), None),
        P(),
    )
    out_specs = (
        P("wshard", None, ("tensor", "dp")),
        P("wshard", None, ("tensor", "dp")),
        P("wshard", None, ("tensor", "dp")),
        P("wshard", ("tensor", "dp"), None),
        P("wshard", None, None),
        P("wshard", None, "tensor"),
        P("wshard", ("tensor", "dp")),
        P("wshard", ("tensor", "dp")),
        P(None, ("tensor", "dp")),
        P(("tensor", "dp"), None),
        P(),
        P("wshard", "tensor"),
    )
    return jax.shard_map(shards, mesh=mesh, in_specs=in_specs, out_specs=out_specs, check_vma=False)
```

```python
import jax
import jax.numpy as jnp
from jax import lax
from jax.sharding import PartitionSpec as P

NS_ITERS = 3


HIGHEST = lax.Precision.HIGHEST
HIGH = lax.Precision.HIGH
linear_coef = 3.4445
cubic_coef = -4.775
quintic_coef = 2.0315


def local_gram(current):
    return jnp.einsum("bki,bkj->bij", current, current, precision=HIGH)


def quintic_step(current, gram_matrix):
    first_prod = jnp.einsum("bik,bkj->bij", current, gram_matrix, precision=HIGH)
    second_prod = jnp.einsum("bik,bkj->bij", first_prod, gram_matrix, precision=HIGH)
    return linear_coef * current + cubic_coef * first_prod + quintic_coef * second_prod


def shards(
    expert_grads,
    dense_grads,
    expert_master,
    expert_first,
    expert_second,
    expert_stat,
    expert_basis,
    dense_master,
    dense_first,
    dense_second,
    dense_stat,
    dense_basis,
):
    replicas = lax.axis_size("dp")
    experts_here = expert_grads.shape[1]
    expert_local = expert_grads.reshape(expert_grads.shape[1:]).astype(jnp.float32)
    dense_local = dense_grads.reshape(dense_grads.shape[1:]).astype(jnp.float32)
    expert_sum, dense_sum = (
        lax.psum_scatter(expert_local, "dp", scatter_dimension=2, tiled=True),
        lax.psum_scatter(dense_local, "dp", scatter_dimension=1, tiled=True),
    )
    expert_mean = expert_sum / replicas
    dense_mean = dense_sum / replicas
    expert_first_out = 0.9 * expert_first + 0.1 * expert_mean
    dense_first_out = 0.9 * dense_first + 0.1 * dense_mean
    dense_grad_full, dense_first_full = (
        lax.all_gather(dense_mean, "wshard", axis=0, tiled=True),
        lax.all_gather(dense_first_out, "wshard", axis=0, tiled=True),
    )
    grads_all = jnp.concatenate([expert_mean, dense_grad_full[None]], 0)
    firsts_all = jnp.concatenate([expert_first_out, dense_first_full[None]], 0)
    bases_all = jnp.concatenate([expert_basis, dense_basis[None]], 0)
    seconds_all = jnp.concatenate([expert_second, dense_second[None]], 0)
    columns = grads_all.shape[2]
    rotated = jnp.einsum(
        "bki,bkc->bic", bases_all, jnp.concatenate([grads_all, firsts_all], 2), precision=HIGHEST
    )
    grad_rot = rotated[:, :, :columns]
    first_rot = rotated[:, :, columns:]
    seconds_out = 0.95 * seconds_all + 0.05 * grad_rot * grad_rot
    scaled = first_rot / (jnp.sqrt(seconds_out) + 1e-08)
    update = jnp.einsum("bik,bkc->bic", bases_all, scaled, precision=HIGHEST)
    expert_master_out = expert_master - 0.05 * update[:experts_here]
    dense_rows_here = dense_master.shape[0]
    dense_update = lax.dynamic_slice_in_dim(
        update[experts_here], lax.axis_index("wshard") * dense_rows_here, dense_rows_here, 0
    )
    dense_master_out = dense_master - 0.05 * dense_update
    expert_weights, dense_weights = (
        lax.all_gather(expert_master_out.astype(jnp.bfloat16), "dp", axis=2, tiled=True),
        lax.all_gather(dense_master_out.astype(jnp.bfloat16), "dp", axis=1, tiled=True),
    )
    partial_stat = jnp.einsum("bic,bjc->bij", grads_all, grads_all, precision=HIGHEST)
    stats_all = jnp.concatenate([expert_stat, dense_stat[None]], 0)
    stat_rows = stats_all.shape[1]
    row_start = lax.axis_index(("tensor", "dp")) * stat_rows
    placed = lax.dynamic_update_slice_in_dim(
        jnp.zeros_like(partial_stat), 0.95 * stats_all, row_start, 1
    )
    stats_full = lax.psum(placed + 0.05 * partial_stat, ("tensor", "dp"))
    stats_out = lax.dynamic_slice_in_dim(stats_full, row_start, stat_rows, 1)
    tensor_size = lax.axis_size("tensor")
    core = lax.axis_index("tensor") % 2
    stat_mine = lax.dynamic_slice_in_dim(stats_full, core, 1, 0)
    basis_mine = lax.dynamic_slice_in_dim(bases_all, core, 1, 0)
    power = jnp.einsum("bik,bkj->bij", stat_mine, basis_mine, precision=HIGH)
    square_sum = jnp.sum(power * power, (1, 2))
    current = power * lax.rsqrt(square_sum + 1e-06)[:, None, None]

    def ns_iteration(repeat, current):
        return quintic_step(current, local_gram(current))

    current = lax.fori_loop(0, NS_ITERS, ns_iteration, current)
    partner = lax.ppermute(
        current, "tensor", perm=[(t, t ^ 1) for t in range(tensor_size)]
    )
    bases_out = jnp.where(
        core == 0,
        jnp.concatenate([current, partner], 0),
        jnp.concatenate([partner, current], 0),
    )
    return (
        expert_master_out,
        expert_first_out,
        seconds_out[:experts_here],
        stats_out[:experts_here],
        bases_out[:experts_here],
        expert_weights,
        dense_master_out,
        dense_first_out,
        seconds_out[experts_here],
        stats_out[experts_here],
        bases_out[experts_here],
        dense_weights,
    )


def solution(mesh):
    in_specs = (
        P("dp", "wshard", None, "tensor"),
        P("dp", "wshard", "tensor"),
        P("wshard", None, ("tensor", "dp")),
        P("wshard", None, ("tensor", "dp")),
        P("wshard", None, ("tensor", "dp")),
        P("wshard", ("tensor", "dp"), None),
        P("wshard", None, None),
        P("wshard", ("tensor", "dp")),
        P("wshard", ("tensor", "dp")),
        P(None, ("tensor", "dp")),
        P(("tensor", "dp"), None),
        P(),
    )
    out_specs = (
        P("wshard", None, ("tensor", "dp")),
        P("wshard", None, ("tensor", "dp")),
        P("wshard", None, ("tensor", "dp")),
        P("wshard", ("tensor", "dp"), None),
        P("wshard", None, None),
        P("wshard", None, "tensor"),
        P("wshard", ("tensor", "dp")),
        P("wshard", ("tensor", "dp")),
        P(None, ("tensor", "dp")),
        P(("tensor", "dp"), None),
        P(),
        P("wshard", "tensor"),
    )
    return jax.shard_map(shards, mesh=mesh, in_specs=in_specs, out_specs=out_specs, check_vma=False)
```

```python
import jax
import jax.numpy as jnp
from jax import lax
from jax.sharding import PartitionSpec as P

NS_ITERS = 3


HIGHEST = lax.Precision.HIGHEST
HIGH = lax.Precision.HIGH
linear_coef = 3.4445
cubic_coef = -4.775
quintic_coef = 2.0315


def local_gram(current):
    return jnp.einsum("bki,bkj->bij", current, current, precision=HIGH)


def quintic_step(current, gram_matrix):
    first_prod = jnp.einsum("bik,bkj->bij", current, gram_matrix, precision=HIGH)
    second_prod = jnp.einsum("bik,bkj->bij", first_prod, gram_matrix, precision=HIGH)
    return linear_coef * current + cubic_coef * first_prod + quintic_coef * second_prod


def shards(
    expert_grads,
    dense_grads,
    expert_master,
    expert_first,
    expert_second,
    expert_stat,
    expert_basis,
    dense_master,
    dense_first,
    dense_second,
    dense_stat,
    dense_basis,
):
    replicas = lax.axis_size("dp")
    experts_here = expert_grads.shape[1]
    expert_local = expert_grads.reshape(expert_grads.shape[1:]).astype(jnp.float32)
    dense_local = dense_grads.reshape(dense_grads.shape[1:]).astype(jnp.float32)
    expert_sum, dense_sum = (
        lax.psum_scatter(expert_local, "dp", scatter_dimension=2, tiled=True),
        lax.psum_scatter(dense_local, "dp", scatter_dimension=1, tiled=True),
    )
    expert_mean = expert_sum / replicas
    dense_mean = dense_sum / replicas
    expert_first_out = 0.9 * expert_first + 0.1 * expert_mean
    dense_first_out = 0.9 * dense_first + 0.1 * dense_mean
    dense_grad_full, dense_first_full = (
        lax.all_gather(dense_mean, "wshard", axis=0, tiled=True),
        lax.all_gather(dense_first_out, "wshard", axis=0, tiled=True),
    )
    grads_all = jnp.concatenate([expert_mean, dense_grad_full[None]], 0)
    firsts_all = jnp.concatenate([expert_first_out, dense_first_full[None]], 0)
    bases_all = jnp.concatenate([expert_basis, dense_basis[None]], 0)
    seconds_all = jnp.concatenate([expert_second, dense_second[None]], 0)
    columns = grads_all.shape[2]
    rotated = jnp.einsum(
        "bki,bkc->bic", bases_all, jnp.concatenate([grads_all, firsts_all], 2), precision=HIGHEST
    )
    grad_rot = rotated[:, :, :columns]
    first_rot = rotated[:, :, columns:]
    seconds_out = 0.95 * seconds_all + 0.05 * grad_rot * grad_rot
    scaled = first_rot / (jnp.sqrt(seconds_out) + 1e-08)
    update = jnp.einsum("bik,bkc->bic", bases_all, scaled, precision=HIGHEST)
    expert_master_out = expert_master - 0.05 * update[:experts_here]
    dense_rows_here = dense_master.shape[0]
    dense_update = lax.dynamic_slice_in_dim(
        update[experts_here], lax.axis_index("wshard") * dense_rows_here, dense_rows_here, 0
    )
    dense_master_out = dense_master - 0.05 * dense_update
    expert_weights, dense_weights = (
        lax.all_gather(expert_master_out.astype(jnp.bfloat16), "dp", axis=2, tiled=True),
        lax.all_gather(dense_master_out.astype(jnp.bfloat16), "dp", axis=1, tiled=True),
    )
    partial_stat = jnp.einsum("bic,bjc->bij", grads_all, grads_all, precision=HIGHEST)
    stats_all = jnp.concatenate([expert_stat, dense_stat[None]], 0)
    stat_rows = stats_all.shape[1]
    row_start = lax.axis_index(("tensor", "dp")) * stat_rows
    placed = lax.dynamic_update_slice_in_dim(
        jnp.zeros_like(partial_stat), 0.95 * stats_all, row_start, 1
    )
    stats_full = lax.psum(placed + 0.05 * partial_stat, ("tensor", "dp"))
    stats_full, expert_weights, dense_weights, expert_master_out, dense_master_out = (
        lax.optimization_barrier(
            (stats_full, expert_weights, dense_weights, expert_master_out, dense_master_out)
        )
    )
    stats_out = lax.dynamic_slice_in_dim(stats_full, row_start, stat_rows, 1)
    tensor_size = lax.axis_size("tensor")
    core = lax.axis_index("tensor") % 2
    stat_mine = lax.dynamic_slice_in_dim(stats_full, core, 1, 0)
    basis_mine = lax.dynamic_slice_in_dim(bases_all, core, 1, 0)
    power = jnp.einsum("bik,bkj->bij", stat_mine, basis_mine, precision=HIGH)
    square_sum = jnp.sum(power * power, (1, 2))
    current = power * lax.rsqrt(square_sum + 1e-06)[:, None, None]

    def ns_iteration(repeat, current):
        return quintic_step(current, local_gram(current))

    current = lax.fori_loop(0, NS_ITERS, ns_iteration, current)
    partner = lax.ppermute(
        current, "tensor", perm=[(t, t ^ 1) for t in range(tensor_size)]
    )
    bases_out = jnp.where(
        core == 0,
        jnp.concatenate([current, partner], 0),
        jnp.concatenate([partner, current], 0),
    )
    return (
        expert_master_out,
        expert_first_out,
        seconds_out[:experts_here],
        stats_out[:experts_here],
        bases_out[:experts_here],
        expert_weights,
        dense_master_out,
        dense_first_out,
        seconds_out[experts_here],
        stats_out[experts_here],
        bases_out[experts_here],
        dense_weights,
    )


def solution(mesh):
    in_specs = (
        P("dp", "wshard", None, "tensor"),
        P("dp", "wshard", "tensor"),
        P("wshard", None, ("tensor", "dp")),
        P("wshard", None, ("tensor", "dp")),
        P("wshard", None, ("tensor", "dp")),
        P("wshard", ("tensor", "dp"), None),
        P("wshard", None, None),
        P("wshard", ("tensor", "dp")),
        P("wshard", ("tensor", "dp")),
        P(None, ("tensor", "dp")),
        P(("tensor", "dp"), None),
        P(),
    )
    out_specs = (
        P("wshard", None, ("tensor", "dp")),
        P("wshard", None, ("tensor", "dp")),
        P("wshard", None, ("tensor", "dp")),
        P("wshard", ("tensor", "dp"), None),
        P("wshard", None, None),
        P("wshard", None, "tensor"),
        P("wshard", ("tensor", "dp")),
        P("wshard", ("tensor", "dp")),
        P(None, ("tensor", "dp")),
        P(("tensor", "dp"), None),
        P(),
        P("wshard", "tensor"),
    )
    return jax.shard_map(shards, mesh=mesh, in_specs=in_specs, out_specs=out_specs, check_vma=False)
```

```python
import jax
import jax.numpy as jnp
from jax import lax
from jax.sharding import PartitionSpec as P

NS_ITERS = 3


HIGHEST = lax.Precision.HIGHEST
HIGH = lax.Precision.HIGH
linear_coef = 3.4445
cubic_coef = -4.775
quintic_coef = 2.0315


def local_gram(current):
    return jnp.einsum("bki,bkj->bij", current, current, precision=HIGH)


def quintic_step(current, gram_matrix):
    first_prod = jnp.einsum("bik,bkj->bij", current, gram_matrix, precision=HIGH)
    second_prod = jnp.einsum("bik,bkj->bij", first_prod, gram_matrix, precision=HIGH)
    return linear_coef * current + cubic_coef * first_prod + quintic_coef * second_prod


def shards(
    expert_grads,
    dense_grads,
    expert_master,
    expert_first,
    expert_second,
    expert_stat,
    expert_basis,
    dense_master,
    dense_first,
    dense_second,
    dense_stat,
    dense_basis,
):
    replicas = lax.axis_size("dp")
    experts_here = expert_grads.shape[1]
    expert_local = expert_grads.reshape(expert_grads.shape[1:]).astype(jnp.float32)
    dense_local = dense_grads.reshape(dense_grads.shape[1:]).astype(jnp.float32)
    expert_rows = expert_local.shape[1]
    joined = jnp.concatenate([expert_local[0], dense_local], 0)
    joined_sum = lax.psum_scatter(joined, "dp", scatter_dimension=1, tiled=True)
    expert_sum = joined_sum[None, :expert_rows]
    dense_sum = joined_sum[expert_rows:]
    expert_mean = expert_sum / replicas
    dense_mean = dense_sum / replicas
    expert_first_out = 0.9 * expert_first + 0.1 * expert_mean
    dense_first_out = 0.9 * dense_first + 0.1 * dense_mean
    dense_grad_full, dense_first_full = (
        lax.all_gather(dense_mean, "wshard", axis=0, tiled=True),
        lax.all_gather(dense_first_out, "wshard", axis=0, tiled=True),
    )
    grads_all = jnp.concatenate([expert_mean, dense_grad_full[None]], 0)
    firsts_all = jnp.concatenate([expert_first_out, dense_first_full[None]], 0)
    bases_all = jnp.concatenate([expert_basis, dense_basis[None]], 0)
    seconds_all = jnp.concatenate([expert_second, dense_second[None]], 0)
    columns = grads_all.shape[2]
    rotated = jnp.einsum(
        "bki,bkc->bic", bases_all, jnp.concatenate([grads_all, firsts_all], 2), precision=HIGHEST
    )
    grad_rot = rotated[:, :, :columns]
    first_rot = rotated[:, :, columns:]
    seconds_out = 0.95 * seconds_all + 0.05 * grad_rot * grad_rot
    scaled = first_rot / (jnp.sqrt(seconds_out) + 1e-08)
    update = jnp.einsum("bik,bkc->bic", bases_all, scaled, precision=HIGHEST)
    expert_master_out = expert_master - 0.05 * update[:experts_here]
    dense_rows_here = dense_master.shape[0]
    dense_update = lax.dynamic_slice_in_dim(
        update[experts_here], lax.axis_index("wshard") * dense_rows_here, dense_rows_here, 0
    )
    dense_master_out = dense_master - 0.05 * dense_update
    expert_weights, dense_weights = (
        lax.all_gather(expert_master_out.astype(jnp.bfloat16), "dp", axis=2, tiled=True),
        lax.all_gather(dense_master_out.astype(jnp.bfloat16), "dp", axis=1, tiled=True),
    )
    partial_stat = jnp.einsum("bic,bjc->bij", grads_all, grads_all, precision=HIGHEST)
    stats_all = jnp.concatenate([expert_stat, dense_stat[None]], 0)
    stat_rows = stats_all.shape[1]
    row_start = lax.axis_index(("tensor", "dp")) * stat_rows
    placed = lax.dynamic_update_slice_in_dim(
        jnp.zeros_like(partial_stat), 0.95 * stats_all, row_start, 1
    )
    stats_full = lax.psum(placed + 0.05 * partial_stat, ("tensor", "dp"))
    stats_full, expert_weights, dense_weights, expert_master_out, dense_master_out = (
        lax.optimization_barrier(
            (stats_full, expert_weights, dense_weights, expert_master_out, dense_master_out)
        )
    )
    stats_out = lax.dynamic_slice_in_dim(stats_full, row_start, stat_rows, 1)
    tensor_size = lax.axis_size("tensor")
    core = lax.axis_index("tensor") % 2
    stat_mine = lax.dynamic_slice_in_dim(stats_full, core, 1, 0)
    basis_mine = lax.dynamic_slice_in_dim(bases_all, core, 1, 0)
    power = jnp.einsum("bik,bkj->bij", stat_mine, basis_mine, precision=HIGH)
    square_sum = jnp.sum(power * power, (1, 2))
    current = power * lax.rsqrt(square_sum + 1e-06)[:, None, None]

    def ns_iteration(repeat, current):
        return quintic_step(current, local_gram(current))

    current = lax.fori_loop(0, NS_ITERS, ns_iteration, current)
    partner = lax.ppermute(
        current, "tensor", perm=[(t, t ^ 1) for t in range(tensor_size)]
    )
    bases_out = jnp.where(
        core == 0,
        jnp.concatenate([current, partner], 0),
        jnp.concatenate([partner, current], 0),
    )
    return (
        expert_master_out,
        expert_first_out,
        seconds_out[:experts_here],
        stats_out[:experts_here],
        bases_out[:experts_here],
        expert_weights,
        dense_master_out,
        dense_first_out,
        seconds_out[experts_here],
        stats_out[experts_here],
        bases_out[experts_here],
        dense_weights,
    )


def solution(mesh):
    in_specs = (
        P("dp", "wshard", None, "tensor"),
        P("dp", "wshard", "tensor"),
        P("wshard", None, ("tensor", "dp")),
        P("wshard", None, ("tensor", "dp")),
        P("wshard", None, ("tensor", "dp")),
        P("wshard", ("tensor", "dp"), None),
        P("wshard", None, None),
        P("wshard", ("tensor", "dp")),
        P("wshard", ("tensor", "dp")),
        P(None, ("tensor", "dp")),
        P(("tensor", "dp"), None),
        P(),
    )
    out_specs = (
        P("wshard", None, ("tensor", "dp")),
        P("wshard", None, ("tensor", "dp")),
        P("wshard", None, ("tensor", "dp")),
        P("wshard", ("tensor", "dp"), None),
        P("wshard", None, None),
        P("wshard", None, "tensor"),
        P("wshard", ("tensor", "dp")),
        P("wshard", ("tensor", "dp")),
        P(None, ("tensor", "dp")),
        P(("tensor", "dp"), None),
        P(),
        P("wshard", "tensor"),
    )
    return jax.shard_map(shards, mesh=mesh, in_specs=in_specs, out_specs=out_specs, check_vma=False)
```

```python
import jax
import jax.numpy as jnp
from jax import lax
from jax.sharding import PartitionSpec as P

NS_ITERS = 3


HIGHEST = lax.Precision.HIGHEST
HIGH = lax.Precision.HIGH
linear_coef = 3.4445
cubic_coef = -4.775
quintic_coef = 2.0315


def local_gram(current):
    return jnp.einsum("bki,bkj->bij", current, current, precision=HIGH)


def quintic_step(current, gram_matrix):
    first_prod = jnp.einsum("bik,bkj->bij", current, gram_matrix, precision=HIGH)
    second_prod = jnp.einsum("bik,bkj->bij", first_prod, gram_matrix, precision=HIGH)
    return linear_coef * current + cubic_coef * first_prod + quintic_coef * second_prod


def shards(
    expert_grads,
    dense_grads,
    expert_master,
    expert_first,
    expert_second,
    expert_stat,
    expert_basis,
    dense_master,
    dense_first,
    dense_second,
    dense_stat,
    dense_basis,
):
    replicas = lax.axis_size("dp")
    experts_here = expert_grads.shape[1]
    expert_local = expert_grads.reshape(expert_grads.shape[2:])
    dense_local = dense_grads.reshape(dense_grads.shape[1:])
    expert_rows = expert_local.shape[0]
    joined = jnp.concatenate([expert_local, dense_local], 0)
    owned = joined.shape[1] // replicas
    joined = joined.reshape(joined.shape[0], replicas, owned).transpose(1, 0, 2)
    received = lax.all_to_all(joined, "dp", 0, 0, tiled=True)
    joined_sum = jnp.sum(received.astype(jnp.float32), 0)
    expert_sum = joined_sum[None, :expert_rows]
    dense_sum = joined_sum[expert_rows:]
    expert_mean = expert_sum / replicas
    dense_mean = dense_sum / replicas
    expert_first_out = 0.9 * expert_first + 0.1 * expert_mean
    dense_first_out = 0.9 * dense_first + 0.1 * dense_mean
    dense_grad_full, dense_first_full = (
        lax.all_gather(dense_mean, "wshard", axis=0, tiled=True),
        lax.all_gather(dense_first_out, "wshard", axis=0, tiled=True),
    )
    grads_all = jnp.concatenate([expert_mean, dense_grad_full[None]], 0)
    firsts_all = jnp.concatenate([expert_first_out, dense_first_full[None]], 0)
    bases_all = jnp.concatenate([expert_basis, dense_basis[None]], 0)
    seconds_all = jnp.concatenate([expert_second, dense_second[None]], 0)
    columns = grads_all.shape[2]
    rotated = jnp.einsum(
        "bki,bkc->bic", bases_all, jnp.concatenate([grads_all, firsts_all], 2), precision=HIGHEST
    )
    grad_rot = rotated[:, :, :columns]
    first_rot = rotated[:, :, columns:]
    seconds_out = 0.95 * seconds_all + 0.05 * grad_rot * grad_rot
    scaled = first_rot / (jnp.sqrt(seconds_out) + 1e-08)
    update = jnp.einsum("bik,bkc->bic", bases_all, scaled, precision=HIGHEST)
    expert_master_out = expert_master - 0.05 * update[:experts_here]
    dense_rows_here = dense_master.shape[0]
    dense_update = lax.dynamic_slice_in_dim(
        update[experts_here], lax.axis_index("wshard") * dense_rows_here, dense_rows_here, 0
    )
    dense_master_out = dense_master - 0.05 * dense_update
    expert_weights, dense_weights = (
        lax.all_gather(expert_master_out.astype(jnp.bfloat16), "dp", axis=2, tiled=True),
        lax.all_gather(dense_master_out.astype(jnp.bfloat16), "dp", axis=1, tiled=True),
    )
    partial_stat = jnp.einsum("bic,bjc->bij", grads_all, grads_all, precision=HIGHEST)
    stats_all = jnp.concatenate([expert_stat, dense_stat[None]], 0)
    stat_rows = stats_all.shape[1]
    row_start = lax.axis_index(("tensor", "dp")) * stat_rows
    placed = lax.dynamic_update_slice_in_dim(
        jnp.zeros_like(partial_stat), 0.95 * stats_all, row_start, 1
    )
    stats_full = lax.psum(placed + 0.05 * partial_stat, ("tensor", "dp"))
    stats_full, expert_weights, dense_weights, expert_master_out, dense_master_out = (
        lax.optimization_barrier(
            (stats_full, expert_weights, dense_weights, expert_master_out, dense_master_out)
        )
    )
    stats_out = lax.dynamic_slice_in_dim(stats_full, row_start, stat_rows, 1)
    tensor_size = lax.axis_size("tensor")
    core = lax.axis_index("tensor") % 2
    stat_mine = lax.dynamic_slice_in_dim(stats_full, core, 1, 0)
    basis_mine = lax.dynamic_slice_in_dim(bases_all, core, 1, 0)
    power = jnp.einsum("bik,bkj->bij", stat_mine, basis_mine, precision=HIGH)
    square_sum = jnp.sum(power * power, (1, 2))
    current = power * lax.rsqrt(square_sum + 1e-06)[:, None, None]

    def ns_iteration(repeat, current):
        return quintic_step(current, local_gram(current))

    current = lax.fori_loop(0, NS_ITERS, ns_iteration, current)
    partner = lax.ppermute(
        current, "tensor", perm=[(t, t ^ 1) for t in range(tensor_size)]
    )
    bases_out = jnp.where(
        core == 0,
        jnp.concatenate([current, partner], 0),
        jnp.concatenate([partner, current], 0),
    )
    return (
        expert_master_out,
        expert_first_out,
        seconds_out[:experts_here],
        stats_out[:experts_here],
        bases_out[:experts_here],
        expert_weights,
        dense_master_out,
        dense_first_out,
        seconds_out[experts_here],
        stats_out[experts_here],
        bases_out[experts_here],
        dense_weights,
    )


def solution(mesh):
    in_specs = (
        P("dp", "wshard", None, "tensor"),
        P("dp", "wshard", "tensor"),
        P("wshard", None, ("tensor", "dp")),
        P("wshard", None, ("tensor", "dp")),
        P("wshard", None, ("tensor", "dp")),
        P("wshard", ("tensor", "dp"), None),
        P("wshard", None, None),
        P("wshard", ("tensor", "dp")),
        P("wshard", ("tensor", "dp")),
        P(None, ("tensor", "dp")),
        P(("tensor", "dp"), None),
        P(),
    )
    out_specs = (
        P("wshard", None, ("tensor", "dp")),
        P("wshard", None, ("tensor", "dp")),
        P("wshard", None, ("tensor", "dp")),
        P("wshard", ("tensor", "dp"), None),
        P("wshard", None, None),
        P("wshard", None, "tensor"),
        P("wshard", ("tensor", "dp")),
        P("wshard", ("tensor", "dp")),
        P(None, ("tensor", "dp")),
        P(("tensor", "dp"), None),
        P(),
        P("wshard", "tensor"),
    )
    return jax.shard_map(shards, mesh=mesh, in_specs=in_specs, out_specs=out_specs, check_vma=False)
```

```python
import jax
import jax.numpy as jnp
from jax import lax
from jax.sharding import PartitionSpec as P

NS_ITERS = 3


HIGHEST = lax.Precision.HIGHEST
HIGH = lax.Precision.HIGH
linear_coef = 3.4445
cubic_coef = -4.775
quintic_coef = 2.0315


def local_gram(current):
    return jnp.einsum("bki,bkj->bij", current, current, precision=HIGH)


def quintic_step(current, gram_matrix):
    first_prod = jnp.einsum("bik,bkj->bij", current, gram_matrix, precision=HIGH)
    second_prod = jnp.einsum("bik,bkj->bij", first_prod, gram_matrix, precision=HIGH)
    return linear_coef * current + cubic_coef * first_prod + quintic_coef * second_prod


def symmetric_psum(full, axes):
    size = full.shape[-1]
    block = 128 if size % 128 == 0 else size
    count = size // block
    strips = [full[:, i * block : (i + 1) * block, i * block :] for i in range(count)]
    summed = lax.psum(jnp.concatenate(strips, 2), axes)
    rows = []
    offset = 0
    for i in range(count):
        width = size - i * block
        strip = summed[:, :, offset : offset + width]
        offset += width
        rows.append(jnp.pad(strip, ((0, 0), (0, 0), (i * block, 0))))
    upper = jnp.concatenate(rows, 1)
    block_index = jnp.arange(size) // block
    strict = block_index[:, None] < block_index[None, :]
    return upper + jnp.swapaxes(jnp.where(strict, upper, 0.0), 1, 2)


def shards(
    expert_grads,
    dense_grads,
    expert_master,
    expert_first,
    expert_second,
    expert_stat,
    expert_basis,
    dense_master,
    dense_first,
    dense_second,
    dense_stat,
    dense_basis,
):
    replicas = lax.axis_size("dp")
    experts_here = expert_grads.shape[1]
    expert_local = expert_grads.reshape(expert_grads.shape[2:])
    dense_local = dense_grads.reshape(dense_grads.shape[1:])
    expert_rows = expert_local.shape[0]
    joined = jnp.concatenate([expert_local, dense_local], 0)
    owned = joined.shape[1] // replicas
    joined = joined.reshape(joined.shape[0], replicas, owned).transpose(1, 0, 2)
    received = lax.all_to_all(joined, "dp", 0, 0, tiled=True)
    joined_sum = jnp.sum(received.astype(jnp.float32), 0)
    expert_sum = joined_sum[None, :expert_rows]
    dense_sum = joined_sum[expert_rows:]
    expert_mean = expert_sum / replicas
    dense_mean = dense_sum / replicas
    expert_first_out = 0.9 * expert_first + 0.1 * expert_mean
    dense_first_out = 0.9 * dense_first + 0.1 * dense_mean
    dense_grad_full, dense_first_full = (
        lax.all_gather(dense_mean, "wshard", axis=0, tiled=True),
        lax.all_gather(dense_first_out, "wshard", axis=0, tiled=True),
    )
    grads_all = jnp.concatenate([expert_mean, dense_grad_full[None]], 0)
    firsts_all = jnp.concatenate([expert_first_out, dense_first_full[None]], 0)
    bases_all = jnp.concatenate([expert_basis, dense_basis[None]], 0)
    seconds_all = jnp.concatenate([expert_second, dense_second[None]], 0)
    columns = grads_all.shape[2]
    rotated = jnp.einsum(
        "bki,bkc->bic", bases_all, jnp.concatenate([grads_all, firsts_all], 2), precision=HIGHEST
    )
    grad_rot = rotated[:, :, :columns]
    first_rot = rotated[:, :, columns:]
    seconds_out = 0.95 * seconds_all + 0.05 * grad_rot * grad_rot
    scaled = first_rot / (jnp.sqrt(seconds_out) + 1e-08)
    update = jnp.einsum("bik,bkc->bic", bases_all, scaled, precision=HIGHEST)
    expert_master_out = expert_master - 0.05 * update[:experts_here]
    dense_rows_here = dense_master.shape[0]
    dense_update = lax.dynamic_slice_in_dim(
        update[experts_here], lax.axis_index("wshard") * dense_rows_here, dense_rows_here, 0
    )
    dense_master_out = dense_master - 0.05 * dense_update
    expert_weights, dense_weights = (
        lax.all_gather(expert_master_out.astype(jnp.bfloat16), "dp", axis=2, tiled=True),
        lax.all_gather(dense_master_out.astype(jnp.bfloat16), "dp", axis=1, tiled=True),
    )
    partial_stat = jnp.einsum("bic,bjc->bij", grads_all, grads_all, precision=HIGHEST)
    stats_all = jnp.concatenate([expert_stat, dense_stat[None]], 0)
    stat_rows = stats_all.shape[1]
    row_start = lax.axis_index(("tensor", "dp")) * stat_rows
    placed = lax.dynamic_update_slice_in_dim(
        jnp.zeros_like(partial_stat), 0.95 * stats_all, row_start, 1
    )
    stats_full = symmetric_psum(placed + 0.05 * partial_stat, ("tensor", "dp"))
    stats_full, expert_weights, dense_weights, expert_master_out, dense_master_out = (
        lax.optimization_barrier(
            (stats_full, expert_weights, dense_weights, expert_master_out, dense_master_out)
        )
    )
    stats_out = lax.dynamic_slice_in_dim(stats_full, row_start, stat_rows, 1)
    tensor_size = lax.axis_size("tensor")
    core = lax.axis_index("tensor") % 2
    stat_mine = lax.dynamic_slice_in_dim(stats_full, core, 1, 0)
    basis_mine = lax.dynamic_slice_in_dim(bases_all, core, 1, 0)
    power = jnp.einsum("bik,bkj->bij", stat_mine, basis_mine, precision=HIGH)
    square_sum = jnp.sum(power * power, (1, 2))
    current = power * lax.rsqrt(square_sum + 1e-06)[:, None, None]

    def ns_iteration(repeat, current):
        return quintic_step(current, local_gram(current))

    current = lax.fori_loop(0, NS_ITERS, ns_iteration, current)
    partner = lax.ppermute(
        current, "tensor", perm=[(t, t ^ 1) for t in range(tensor_size)]
    )
    bases_out = jnp.where(
        core == 0,
        jnp.concatenate([current, partner], 0),
        jnp.concatenate([partner, current], 0),
    )
    return (
        expert_master_out,
        expert_first_out,
        seconds_out[:experts_here],
        stats_out[:experts_here],
        bases_out[:experts_here],
        expert_weights,
        dense_master_out,
        dense_first_out,
        seconds_out[experts_here],
        stats_out[experts_here],
        bases_out[experts_here],
        dense_weights,
    )


def solution(mesh):
    in_specs = (
        P("dp", "wshard", None, "tensor"),
        P("dp", "wshard", "tensor"),
        P("wshard", None, ("tensor", "dp")),
        P("wshard", None, ("tensor", "dp")),
        P("wshard", None, ("tensor", "dp")),
        P("wshard", ("tensor", "dp"), None),
        P("wshard", None, None),
        P("wshard", ("tensor", "dp")),
        P("wshard", ("tensor", "dp")),
        P(None, ("tensor", "dp")),
        P(("tensor", "dp"), None),
        P(),
    )
    out_specs = (
        P("wshard", None, ("tensor", "dp")),
        P("wshard", None, ("tensor", "dp")),
        P("wshard", None, ("tensor", "dp")),
        P("wshard", ("tensor", "dp"), None),
        P("wshard", None, None),
        P("wshard", None, "tensor"),
        P("wshard", ("tensor", "dp")),
        P("wshard", ("tensor", "dp")),
        P(None, ("tensor", "dp")),
        P(("tensor", "dp"), None),
        P(),
        P("wshard", "tensor"),
    )
    return jax.shard_map(shards, mesh=mesh, in_specs=in_specs, out_specs=out_specs, check_vma=False)
```

```python
import jax
import jax.numpy as jnp
from jax import lax
from jax.sharding import PartitionSpec as P

NS_ITERS = 3


HIGHEST = lax.Precision.HIGHEST
HIGH = lax.Precision.HIGH
linear_coef = 3.4445
cubic_coef = -4.775
quintic_coef = 2.0315


def local_gram(current):
    return jnp.einsum("bki,bkj->bij", current, current, precision=HIGH)


def quintic_step(current, gram_matrix):
    first_prod = jnp.einsum("bik,bkj->bij", current, gram_matrix, precision=HIGH)
    second_prod = jnp.einsum("bik,bkj->bij", first_prod, gram_matrix, precision=HIGH)
    return linear_coef * current + cubic_coef * first_prod + quintic_coef * second_prod


def shards(
    expert_grads,
    dense_grads,
    expert_master,
    expert_first,
    expert_second,
    expert_stat,
    expert_basis,
    dense_master,
    dense_first,
    dense_second,
    dense_stat,
    dense_basis,
):
    replicas = lax.axis_size("dp")
    experts_here = expert_grads.shape[1]
    expert_local = expert_grads.reshape(expert_grads.shape[2:])
    dense_local = dense_grads.reshape(dense_grads.shape[1:])
    expert_rows = expert_local.shape[0]
    joined = jnp.concatenate([expert_local, dense_local], 0)
    owned = joined.shape[1] // replicas
    joined = joined.reshape(joined.shape[0], replicas, owned).transpose(1, 0, 2)
    received = lax.all_to_all(joined, "dp", 0, 0, tiled=True)
    joined_sum = jnp.sum(received.astype(jnp.float32), 0)
    expert_sum = joined_sum[None, :expert_rows]
    dense_sum = joined_sum[expert_rows:]
    expert_mean = expert_sum / replicas
    dense_mean = dense_sum / replicas
    expert_first_out = 0.9 * expert_first + 0.1 * expert_mean
    dense_first_out = 0.9 * dense_first + 0.1 * dense_mean
    dense_grad_full, dense_first_full = (
        lax.all_gather(dense_mean, "wshard", axis=0, tiled=True),
        lax.all_gather(dense_first_out, "wshard", axis=0, tiled=True),
    )
    grads_all = jnp.concatenate([expert_mean, dense_grad_full[None]], 0)
    firsts_all = jnp.concatenate([expert_first_out, dense_first_full[None]], 0)
    bases_all = jnp.concatenate([expert_basis, dense_basis[None]], 0)
    seconds_all = jnp.concatenate([expert_second, dense_second[None]], 0)
    columns = grads_all.shape[2]
    rotated = jnp.einsum(
        "bki,bkc->bic", bases_all, jnp.concatenate([grads_all, firsts_all], 2), precision=HIGHEST
    )
    grad_rot = rotated[:, :, :columns]
    first_rot = rotated[:, :, columns:]
    seconds_out = 0.95 * seconds_all + 0.05 * grad_rot * grad_rot
    scaled = first_rot / (jnp.sqrt(seconds_out) + 1e-08)
    update = jnp.einsum("bik,bkc->bic", bases_all, scaled, precision=HIGHEST)
    expert_master_out = expert_master - 0.05 * update[:experts_here]
    dense_rows_here = dense_master.shape[0]
    dense_update = lax.dynamic_slice_in_dim(
        update[experts_here], lax.axis_index("wshard") * dense_rows_here, dense_rows_here, 0
    )
    dense_master_out = dense_master - 0.05 * dense_update
    expert_weights, dense_weights = (
        lax.all_gather(expert_master_out.astype(jnp.bfloat16), "dp", axis=2, tiled=True),
        lax.all_gather(dense_master_out.astype(jnp.bfloat16), "dp", axis=1, tiled=True),
    )
    partial_stat = jnp.einsum("bic,bjc->bij", grads_all, grads_all, precision=HIGHEST)
    stats_all = jnp.concatenate([expert_stat, dense_stat[None]], 0)
    stat_rows = stats_all.shape[1]
    row_start = lax.axis_index(("tensor", "dp")) * stat_rows
    placed = lax.dynamic_update_slice_in_dim(
        jnp.zeros_like(partial_stat), 0.95 * stats_all, row_start, 1
    )
    stats_full = lax.psum(lax.psum(placed + 0.05 * partial_stat, "dp"), "tensor")
    stats_full, expert_weights, dense_weights, expert_master_out, dense_master_out = (
        lax.optimization_barrier(
            (stats_full, expert_weights, dense_weights, expert_master_out, dense_master_out)
        )
    )
    stats_out = lax.dynamic_slice_in_dim(stats_full, row_start, stat_rows, 1)
    tensor_size = lax.axis_size("tensor")
    core = lax.axis_index("tensor") % 2
    stat_mine = lax.dynamic_slice_in_dim(stats_full, core, 1, 0)
    basis_mine = lax.dynamic_slice_in_dim(bases_all, core, 1, 0)
    power = jnp.einsum("bik,bkj->bij", stat_mine, basis_mine, precision=HIGH)
    square_sum = jnp.sum(power * power, (1, 2))
    current = power * lax.rsqrt(square_sum + 1e-06)[:, None, None]

    def ns_iteration(repeat, current):
        return quintic_step(current, local_gram(current))

    current = lax.fori_loop(0, NS_ITERS, ns_iteration, current)
    partner = lax.ppermute(
        current, "tensor", perm=[(t, t ^ 1) for t in range(tensor_size)]
    )
    bases_out = jnp.where(
        core == 0,
        jnp.concatenate([current, partner], 0),
        jnp.concatenate([partner, current], 0),
    )
    return (
        expert_master_out,
        expert_first_out,
        seconds_out[:experts_here],
        stats_out[:experts_here],
        bases_out[:experts_here],
        expert_weights,
        dense_master_out,
        dense_first_out,
        seconds_out[experts_here],
        stats_out[experts_here],
        bases_out[experts_here],
        dense_weights,
    )


def solution(mesh):
    in_specs = (
        P("dp", "wshard", None, "tensor"),
        P("dp", "wshard", "tensor"),
        P("wshard", None, ("tensor", "dp")),
        P("wshard", None, ("tensor", "dp")),
        P("wshard", None, ("tensor", "dp")),
        P("wshard", ("tensor", "dp"), None),
        P("wshard", None, None),
        P("wshard", ("tensor", "dp")),
        P("wshard", ("tensor", "dp")),
        P(None, ("tensor", "dp")),
        P(("tensor", "dp"), None),
        P(),
    )
    out_specs = (
        P("wshard", None, ("tensor", "dp")),
        P("wshard", None, ("tensor", "dp")),
        P("wshard", None, ("tensor", "dp")),
        P("wshard", ("tensor", "dp"), None),
        P("wshard", None, None),
        P("wshard", None, "tensor"),
        P("wshard", ("tensor", "dp")),
        P("wshard", ("tensor", "dp")),
        P(None, ("tensor", "dp")),
        P(("tensor", "dp"), None),
        P(),
        P("wshard", "tensor"),
    )
    return jax.shard_map(shards, mesh=mesh, in_specs=in_specs, out_specs=out_specs, check_vma=False)
```

```python
import jax
import jax.numpy as jnp
from jax import lax
from jax.sharding import PartitionSpec as P

NS_ITERS = 3


HIGHEST = lax.Precision.HIGHEST
HIGH = lax.Precision.HIGH
linear_coef = 3.4445
cubic_coef = -4.775
quintic_coef = 2.0315


def local_gram(current):
    return jnp.einsum("bik,bjk->bij", current, current, precision=HIGH)


def quintic_step(current, gram_matrix):
    first_prod = jnp.einsum("bik,bkj->bij", gram_matrix, current, precision=HIGH)
    second_prod = jnp.einsum("bik,bkj->bij", gram_matrix, first_prod, precision=HIGH)
    return linear_coef * current + cubic_coef * first_prod + quintic_coef * second_prod


def shards(
    expert_grads,
    dense_grads,
    expert_master,
    expert_first,
    expert_second,
    expert_stat,
    expert_basis,
    dense_master,
    dense_first,
    dense_second,
    dense_stat,
    dense_basis,
):
    replicas = lax.axis_size("dp")
    experts_here = expert_grads.shape[1]
    expert_local = expert_grads.reshape(expert_grads.shape[2:])
    dense_local = dense_grads.reshape(dense_grads.shape[1:])
    expert_rows = expert_local.shape[0]
    joined = jnp.concatenate([expert_local, dense_local], 0)
    owned = joined.shape[1] // replicas
    joined = joined.reshape(joined.shape[0], replicas, owned).transpose(1, 0, 2)
    received = lax.all_to_all(joined, "dp", 0, 0, tiled=True)
    joined_sum = jnp.sum(received.astype(jnp.float32), 0)
    expert_sum = joined_sum[None, :expert_rows]
    dense_sum = joined_sum[expert_rows:]
    expert_mean = expert_sum / replicas
    dense_mean = dense_sum / replicas
    expert_first_out = 0.9 * expert_first + 0.1 * expert_mean
    dense_first_out = 0.9 * dense_first + 0.1 * dense_mean
    dense_grad_full, dense_first_full = (
        lax.all_gather(dense_mean, "wshard", axis=0, tiled=True),
        lax.all_gather(dense_first_out, "wshard", axis=0, tiled=True),
    )
    grads_all = jnp.concatenate([expert_mean, dense_grad_full[None]], 0)
    firsts_all = jnp.concatenate([expert_first_out, dense_first_full[None]], 0)
    bases_all = jnp.concatenate([expert_basis, dense_basis[None]], 0)
    seconds_all = jnp.concatenate([expert_second, dense_second[None]], 0)
    columns = grads_all.shape[2]
    rotated = jnp.einsum(
        "bki,bkc->bic", bases_all, jnp.concatenate([grads_all, firsts_all], 2), precision=HIGHEST
    )
    grad_rot = rotated[:, :, :columns]
    first_rot = rotated[:, :, columns:]
    seconds_out = 0.95 * seconds_all + 0.05 * grad_rot * grad_rot
    scaled = first_rot / (jnp.sqrt(seconds_out) + 1e-08)
    update = jnp.einsum("bik,bkc->bic", bases_all, scaled, precision=HIGHEST)
    expert_master_out = expert_master - 0.05 * update[:experts_here]
    dense_rows_here = dense_master.shape[0]
    dense_update = lax.dynamic_slice_in_dim(
        update[experts_here], lax.axis_index("wshard") * dense_rows_here, dense_rows_here, 0
    )
    dense_master_out = dense_master - 0.05 * dense_update
    expert_weights, dense_weights = (
        lax.all_gather(expert_master_out.astype(jnp.bfloat16), "dp", axis=2, tiled=True),
        lax.all_gather(dense_master_out.astype(jnp.bfloat16), "dp", axis=1, tiled=True),
    )
    partial_stat = jnp.einsum("bic,bjc->bij", grads_all, grads_all, precision=HIGHEST)
    stats_all = jnp.concatenate([expert_stat, dense_stat[None]], 0)
    stat_rows = stats_all.shape[1]
    row_start = lax.axis_index(("tensor", "dp")) * stat_rows
    placed = lax.dynamic_update_slice_in_dim(
        jnp.zeros_like(partial_stat), 0.95 * stats_all, row_start, 1
    )
    stats_full = lax.psum(placed + 0.05 * partial_stat, ("tensor", "dp"))
    stats_full, expert_weights, dense_weights, expert_master_out, dense_master_out = (
        lax.optimization_barrier(
            (stats_full, expert_weights, dense_weights, expert_master_out, dense_master_out)
        )
    )
    stats_out = lax.dynamic_slice_in_dim(stats_full, row_start, stat_rows, 1)
    tensor_size = lax.axis_size("tensor")
    core = lax.axis_index("tensor") % 2
    stat_mine = lax.dynamic_slice_in_dim(stats_full, core, 1, 0)
    basis_mine = lax.dynamic_slice_in_dim(bases_all, core, 1, 0)
    power = jnp.einsum("bik,bkj->bij", stat_mine, basis_mine, precision=HIGH)
    square_sum = jnp.sum(power * power, (1, 2))
    current = power * lax.rsqrt(square_sum + 1e-06)[:, None, None]

    def ns_iteration(repeat, current):
        return quintic_step(current, local_gram(current))

    current = lax.fori_loop(0, NS_ITERS, ns_iteration, current)
    partner = lax.ppermute(
        current, "tensor", perm=[(t, t ^ 1) for t in range(tensor_size)]
    )
    expert_basis_out = jnp.where(core == 0, current, partner)
    dense_basis_out = jnp.where(core == 0, partner, current)[0]
    return (
        expert_master_out,
        expert_first_out,
        seconds_out[:experts_here],
        stats_out[:experts_here],
        expert_basis_out,
        expert_weights,
        dense_master_out,
        dense_first_out,
        seconds_out[experts_here],
        stats_out[experts_here],
        dense_basis_out,
        dense_weights,
    )


def solution(mesh):
    in_specs = (
        P("dp", "wshard", None, "tensor"),
        P("dp", "wshard", "tensor"),
        P("wshard", None, ("tensor", "dp")),
        P("wshard", None, ("tensor", "dp")),
        P("wshard", None, ("tensor", "dp")),
        P("wshard", ("tensor", "dp"), None),
        P("wshard", None, None),
        P("wshard", ("tensor", "dp")),
        P("wshard", ("tensor", "dp")),
        P(None, ("tensor", "dp")),
        P(("tensor", "dp"), None),
        P(),
    )
    out_specs = (
        P("wshard", None, ("tensor", "dp")),
        P("wshard", None, ("tensor", "dp")),
        P("wshard", None, ("tensor", "dp")),
        P("wshard", ("tensor", "dp"), None),
        P("wshard", None, None),
        P("wshard", None, "tensor"),
        P("wshard", ("tensor", "dp")),
        P("wshard", ("tensor", "dp")),
        P(None, ("tensor", "dp")),
        P(("tensor", "dp"), None),
        P(),
        P("wshard", "tensor"),
    )
    return jax.shard_map(shards, mesh=mesh, in_specs=in_specs, out_specs=out_specs, check_vma=False)
```

```python
import jax
import jax.numpy as jnp
from jax import lax
from jax.sharding import PartitionSpec as P

NS_ITERS = 3


HIGHEST = lax.Precision.HIGHEST
HIGH = lax.Precision.HIGH
linear_coef = 3.4445
cubic_coef = -4.775
quintic_coef = 2.0315


def local_gram(current):
    return jnp.einsum("bik,bjk->bij", current, current, precision=HIGH)


def quintic_step(current, gram_matrix):
    first_prod = jnp.einsum("bik,bkj->bij", gram_matrix, current, precision=HIGH)
    second_prod = jnp.einsum("bik,bkj->bij", gram_matrix, first_prod, precision=HIGH)
    return linear_coef * current + cubic_coef * first_prod + quintic_coef * second_prod


def gather_rows(block, axis):
    size = lax.axis_size(axis)
    here = lax.axis_index(axis)
    rows = block.shape[0]
    full = jnp.zeros((size * rows,) + block.shape[1:], block.dtype)
    full = lax.dynamic_update_slice_in_dim(full, block, here * rows, 0)
    for shift in range(1, size):
        moved = lax.ppermute(block, axis, perm=[(i, (i + shift) % size) for i in range(size)])
        source = (here - shift) % size
        full = lax.dynamic_update_slice_in_dim(full, moved, source * rows, 0)
    return full


def shards(
    expert_grads,
    dense_grads,
    expert_master,
    expert_first,
    expert_second,
    expert_stat,
    expert_basis,
    dense_master,
    dense_first,
    dense_second,
    dense_stat,
    dense_basis,
):
    replicas = lax.axis_size("dp")
    experts_here = expert_grads.shape[1]
    expert_local = expert_grads.reshape(expert_grads.shape[2:])
    dense_local = dense_grads.reshape(dense_grads.shape[1:])
    expert_rows = expert_local.shape[0]
    joined = jnp.concatenate([expert_local, dense_local], 0)
    owned = joined.shape[1] // replicas
    joined = joined.reshape(joined.shape[0], replicas, owned).transpose(1, 0, 2)
    received = lax.all_to_all(joined, "dp", 0, 0, tiled=True)
    joined_sum = jnp.sum(received.astype(jnp.float32), 0)
    expert_sum = joined_sum[None, :expert_rows]
    dense_sum = joined_sum[expert_rows:]
    expert_mean = expert_sum / replicas
    dense_mean = dense_sum / replicas
    expert_first_out = 0.9 * expert_first + 0.1 * expert_mean
    dense_first_out = 0.9 * dense_first + 0.1 * dense_mean
    dense_grad_full = gather_rows(dense_mean, "wshard")
    dense_first_full = lax.all_gather(dense_first_out, "wshard", axis=0, tiled=True)
    grads_all = jnp.concatenate([expert_mean, dense_grad_full[None]], 0)
    firsts_all = jnp.concatenate([expert_first_out, dense_first_full[None]], 0)
    bases_all = jnp.concatenate([expert_basis, dense_basis[None]], 0)
    seconds_all = jnp.concatenate([expert_second, dense_second[None]], 0)
    columns = grads_all.shape[2]
    rotated = jnp.einsum(
        "bki,bkc->bic", bases_all, jnp.concatenate([grads_all, firsts_all], 2), precision=HIGHEST
    )
    grad_rot = rotated[:, :, :columns]
    first_rot = rotated[:, :, columns:]
    seconds_out = 0.95 * seconds_all + 0.05 * grad_rot * grad_rot
    scaled = first_rot / (jnp.sqrt(seconds_out) + 1e-08)
    update = jnp.einsum("bik,bkc->bic", bases_all, scaled, precision=HIGHEST)
    expert_master_out = expert_master - 0.05 * update[:experts_here]
    dense_rows_here = dense_master.shape[0]
    dense_update = lax.dynamic_slice_in_dim(
        update[experts_here], lax.axis_index("wshard") * dense_rows_here, dense_rows_here, 0
    )
    dense_master_out = dense_master - 0.05 * dense_update
    expert_weights, dense_weights = (
        lax.all_gather(expert_master_out.astype(jnp.bfloat16), "dp", axis=2, tiled=True),
        lax.all_gather(dense_master_out.astype(jnp.bfloat16), "dp", axis=1, tiled=True),
    )
    partial_stat = jnp.concatenate(
        [
            jnp.einsum("bic,bjc->bij", expert_mean, expert_mean, precision=HIGHEST),
            jnp.einsum("ic,jc->ij", dense_grad_full, dense_grad_full, precision=HIGHEST)[None],
        ],
        0,
    )
    stats_all = jnp.concatenate([expert_stat, dense_stat[None]], 0)
    stat_rows = stats_all.shape[1]
    row_start = lax.axis_index(("tensor", "dp")) * stat_rows
    placed = lax.dynamic_update_slice_in_dim(
        jnp.zeros_like(partial_stat), 0.95 * stats_all, row_start, 1
    )
    stats_full = lax.psum(placed + 0.05 * partial_stat, ("tensor", "dp"))
    stats_full, expert_weights, dense_weights, expert_master_out, dense_master_out = (
        lax.optimization_barrier(
            (stats_full, expert_weights, dense_weights, expert_master_out, dense_master_out)
        )
    )
    stats_out = lax.dynamic_slice_in_dim(stats_full, row_start, stat_rows, 1)
    tensor_size = lax.axis_size("tensor")
    core = lax.axis_index("tensor") % 2
    stat_mine = lax.dynamic_slice_in_dim(stats_full, core, 1, 0)
    basis_mine = lax.dynamic_slice_in_dim(bases_all, core, 1, 0)
    power = jnp.einsum("bik,bkj->bij", stat_mine, basis_mine, precision=HIGH)
    square_sum = jnp.sum(power * power, (1, 2))
    current = power * lax.rsqrt(square_sum + 1e-06)[:, None, None]

    def ns_iteration(repeat, current):
        return quintic_step(current, local_gram(current))

    current = lax.fori_loop(0, NS_ITERS, ns_iteration, current)
    partner = lax.ppermute(
        current, "tensor", perm=[(t, t ^ 1) for t in range(tensor_size)]
    )
    expert_basis_out = jnp.where(core == 0, current, partner)
    dense_basis_out = jnp.where(core == 0, partner, current)[0]
    return (
        expert_master_out,
        expert_first_out,
        seconds_out[:experts_here],
        stats_out[:experts_here],
        expert_basis_out,
        expert_weights,
        dense_master_out,
        dense_first_out,
        seconds_out[experts_here],
        stats_out[experts_here],
        dense_basis_out,
        dense_weights,
    )


def solution(mesh):
    in_specs = (
        P("dp", "wshard", None, "tensor"),
        P("dp", "wshard", "tensor"),
        P("wshard", None, ("tensor", "dp")),
        P("wshard", None, ("tensor", "dp")),
        P("wshard", None, ("tensor", "dp")),
        P("wshard", ("tensor", "dp"), None),
        P("wshard", None, None),
        P("wshard", ("tensor", "dp")),
        P("wshard", ("tensor", "dp")),
        P(None, ("tensor", "dp")),
        P(("tensor", "dp"), None),
        P(),
    )
    out_specs = (
        P("wshard", None, ("tensor", "dp")),
        P("wshard", None, ("tensor", "dp")),
        P("wshard", None, ("tensor", "dp")),
        P("wshard", ("tensor", "dp"), None),
        P("wshard", None, None),
        P("wshard", None, "tensor"),
        P("wshard", ("tensor", "dp")),
        P("wshard", ("tensor", "dp")),
        P(None, ("tensor", "dp")),
        P(("tensor", "dp"), None),
        P(),
        P("wshard", "tensor"),
    )
    return jax.shard_map(shards, mesh=mesh, in_specs=in_specs, out_specs=out_specs, check_vma=False)
```

```python
import jax
import jax.numpy as jnp
from jax import lax
from jax.sharding import PartitionSpec as P

NS_ITERS = 3


HIGHEST = lax.Precision.HIGHEST
HIGH = lax.Precision.HIGH
linear_coef = 3.4445
cubic_coef = -4.775
quintic_coef = 2.0315


def local_gram(current):
    return jnp.einsum("bik,bjk->bij", current, current, precision=HIGH)


def quintic_step(current, gram_matrix):
    first_prod = jnp.einsum("bik,bkj->bij", gram_matrix, current, precision=HIGH)
    second_prod = jnp.einsum("bik,bkj->bij", gram_matrix, first_prod, precision=HIGH)
    return linear_coef * current + cubic_coef * first_prod + quintic_coef * second_prod


def gather_rows(block, axis):
    size = lax.axis_size(axis)
    here = lax.axis_index(axis)
    rows = block.shape[0]
    full = jnp.zeros((size * rows,) + block.shape[1:], block.dtype)
    full = lax.dynamic_update_slice_in_dim(full, block, here * rows, 0)
    for shift in range(1, size):
        moved = lax.ppermute(block, axis, perm=[(i, (i + shift) % size) for i in range(size)])
        source = (here - shift) % size
        full = lax.dynamic_update_slice_in_dim(full, moved, source * rows, 0)
    return full


def shards(
    expert_grads,
    dense_grads,
    expert_master,
    expert_first,
    expert_second,
    expert_stat,
    expert_basis,
    dense_master,
    dense_first,
    dense_second,
    dense_stat,
    dense_basis,
):
    replicas = lax.axis_size("dp")
    experts_here = expert_grads.shape[1]
    expert_local = expert_grads.reshape(expert_grads.shape[2:])
    dense_local = dense_grads.reshape(dense_grads.shape[1:])
    expert_rows = expert_local.shape[0]
    joined = jnp.concatenate([expert_local, dense_local], 0)
    owned = joined.shape[1] // replicas
    joined = joined.reshape(joined.shape[0], replicas, owned).transpose(1, 0, 2)
    received = lax.all_to_all(joined, "dp", 0, 0, tiled=True)
    joined_sum = jnp.sum(received.astype(jnp.float32), 0)
    expert_sum = joined_sum[None, :expert_rows]
    dense_sum = joined_sum[expert_rows:]
    expert_mean = expert_sum / replicas
    dense_mean = dense_sum / replicas
    expert_first_out = 0.9 * expert_first + 0.1 * expert_mean
    dense_first_out = 0.9 * dense_first + 0.1 * dense_mean
    dense_grad_full = gather_rows(dense_mean, "wshard")
    dense_first_full = lax.all_gather(dense_first_out, "wshard", axis=0, tiled=True)
    grads_all = jnp.concatenate([expert_mean, dense_grad_full[None]], 0)
    firsts_all = jnp.concatenate([expert_first_out, dense_first_full[None]], 0)
    bases_all = jnp.concatenate([expert_basis, dense_basis[None]], 0)
    seconds_all = jnp.concatenate([expert_second, dense_second[None]], 0)
    columns = grads_all.shape[2]
    rotated = jnp.einsum(
        "bki,bkc->bic", bases_all, jnp.concatenate([grads_all, firsts_all], 2), precision=HIGHEST
    )
    grad_rot = rotated[:, :, :columns]
    first_rot = rotated[:, :, columns:]
    seconds_out = 0.95 * seconds_all + 0.05 * grad_rot * grad_rot
    scaled = first_rot / (jnp.sqrt(seconds_out) + 1e-08)
    update = jnp.einsum("bik,bkc->bic", bases_all, scaled, precision=HIGHEST)
    expert_master_out = expert_master - 0.05 * update[:experts_here]
    dense_rows_here = dense_master.shape[0]
    dense_update = lax.dynamic_slice_in_dim(
        update[experts_here], lax.axis_index("wshard") * dense_rows_here, dense_rows_here, 0
    )
    dense_master_out = dense_master - 0.05 * dense_update
    expert_weights, dense_weights = (
        lax.all_gather(expert_master_out.astype(jnp.bfloat16), "dp", axis=2, tiled=True),
        lax.all_gather(dense_master_out.astype(jnp.bfloat16), "dp", axis=1, tiled=True),
    )
    partial_stat = jnp.concatenate(
        [
            jnp.einsum("bic,bjc->bij", expert_mean, expert_mean, precision=HIGHEST),
            jnp.einsum("ic,jc->ij", dense_grad_full, dense_grad_full, precision=HIGHEST)[None],
        ],
        0,
    )
    stats_all = jnp.concatenate([expert_stat, dense_stat[None]], 0)
    stat_rows = stats_all.shape[1]
    row_start = lax.axis_index(("tensor", "dp")) * stat_rows
    placed = lax.dynamic_update_slice_in_dim(
        jnp.zeros_like(partial_stat), 0.95 * stats_all, row_start, 1
    )
    stats_full = lax.psum(placed + 0.05 * partial_stat, ("tensor", "dp"))
    stats_full, expert_weights, dense_weights, expert_master_out, dense_master_out = (
        lax.optimization_barrier(
            (stats_full, expert_weights, dense_weights, expert_master_out, dense_master_out)
        )
    )
    stats_out = lax.dynamic_slice_in_dim(stats_full, row_start, stat_rows, 1)
    tensor_size = lax.axis_size("tensor")
    core = lax.axis_index("tensor") % 2
    stat_mine = lax.dynamic_slice_in_dim(stats_full, core, 1, 0)
    basis_mine = lax.dynamic_slice_in_dim(bases_all, core, 1, 0)
    power = lax.optimization_barrier(
        jnp.einsum("bik,bkj->bij", stat_mine, basis_mine, precision=HIGH)
    )
    square_sum = jnp.sum(power * power, (1, 2))
    current = power * lax.rsqrt(square_sum + 1e-06)[:, None, None]

    def ns_iteration(repeat, current):
        return quintic_step(current, local_gram(current))

    current = lax.fori_loop(0, NS_ITERS, ns_iteration, current)
    partner = lax.ppermute(
        current, "tensor", perm=[(t, t ^ 1) for t in range(tensor_size)]
    )
    expert_basis_out = jnp.where(core == 0, current, partner)
    dense_basis_out = jnp.where(core == 0, partner, current)[0]
    return (
        expert_master_out,
        expert_first_out,
        seconds_out[:experts_here],
        stats_out[:experts_here],
        expert_basis_out,
        expert_weights,
        dense_master_out,
        dense_first_out,
        seconds_out[experts_here],
        stats_out[experts_here],
        dense_basis_out,
        dense_weights,
    )


def solution(mesh):
    in_specs = (
        P("dp", "wshard", None, "tensor"),
        P("dp", "wshard", "tensor"),
        P("wshard", None, ("tensor", "dp")),
        P("wshard", None, ("tensor", "dp")),
        P("wshard", None, ("tensor", "dp")),
        P("wshard", ("tensor", "dp"), None),
        P("wshard", None, None),
        P("wshard", ("tensor", "dp")),
        P("wshard", ("tensor", "dp")),
        P(None, ("tensor", "dp")),
        P(("tensor", "dp"), None),
        P(),
    )
    out_specs = (
        P("wshard", None, ("tensor", "dp")),
        P("wshard", None, ("tensor", "dp")),
        P("wshard", None, ("tensor", "dp")),
        P("wshard", ("tensor", "dp"), None),
        P("wshard", None, None),
        P("wshard", None, "tensor"),
        P("wshard", ("tensor", "dp")),
        P("wshard", ("tensor", "dp")),
        P(None, ("tensor", "dp")),
        P(("tensor", "dp"), None),
        P(),
        P("wshard", "tensor"),
    )
    return jax.shard_map(shards, mesh=mesh, in_specs=in_specs, out_specs=out_specs, check_vma=False)
```

```python
import jax
import jax.numpy as jnp
from jax import lax
from jax.sharding import PartitionSpec as P

NS_ITERS = 3


HIGHEST = lax.Precision.HIGHEST
HIGH = lax.Precision.HIGH
linear_coef = 3.4445
cubic_coef = -4.775
quintic_coef = 2.0315


def local_gram(current):
    return jnp.einsum("bik,bjk->bij", current, current, precision=HIGH)


def quintic_step(current, gram_matrix):
    first_prod = jnp.einsum("bik,bkj->bij", gram_matrix, current, precision=HIGH)
    second_prod = jnp.einsum("bik,bkj->bij", gram_matrix, first_prod, precision=HIGH)
    return linear_coef * current + cubic_coef * first_prod + quintic_coef * second_prod


def gather_rows(block, axis):
    size = lax.axis_size(axis)
    here = lax.axis_index(axis)
    rows = block.shape[0]
    full = jnp.zeros((size * rows,) + block.shape[1:], block.dtype)
    full = lax.dynamic_update_slice_in_dim(full, block, here * rows, 0)
    for shift in range(1, size):
        moved = lax.ppermute(block, axis, perm=[(i, (i + shift) % size) for i in range(size)])
        source = (here - shift) % size
        full = lax.dynamic_update_slice_in_dim(full, moved, source * rows, 0)
    return full


def shards(
    expert_grads,
    dense_grads,
    expert_master,
    expert_first,
    expert_second,
    expert_stat,
    expert_basis,
    dense_master,
    dense_first,
    dense_second,
    dense_stat,
    dense_basis,
):
    replicas = lax.axis_size("dp")
    experts_here = expert_grads.shape[1]
    expert_local = expert_grads.reshape(expert_grads.shape[2:])
    dense_local = dense_grads.reshape(dense_grads.shape[1:])
    expert_rows = expert_local.shape[0]
    joined = jnp.concatenate([expert_local, dense_local], 0)
    owned = joined.shape[1] // replicas
    joined = joined.reshape(joined.shape[0], replicas, owned).transpose(1, 0, 2)
    here = lax.axis_index("dp")
    joined_sum = lax.dynamic_index_in_dim(joined, here, 0, keepdims=False).astype(jnp.float32)
    for shift in range(1, replicas):
        outgoing = lax.dynamic_index_in_dim(joined, (here + shift) % replicas, 0, keepdims=False)
        incoming = lax.ppermute(
            outgoing, "dp", perm=[(i, (i + shift) % replicas) for i in range(replicas)]
        )
        joined_sum = joined_sum + incoming.astype(jnp.float32)
    expert_sum = joined_sum[None, :expert_rows]
    dense_sum = joined_sum[expert_rows:]
    expert_mean = expert_sum / replicas
    dense_mean = dense_sum / replicas
    expert_first_out = 0.9 * expert_first + 0.1 * expert_mean
    dense_first_out = 0.9 * dense_first + 0.1 * dense_mean
    dense_grad_full = gather_rows(dense_mean, "wshard")
    dense_first_full = lax.all_gather(dense_first_out, "wshard", axis=0, tiled=True)
    grads_all = jnp.concatenate([expert_mean, dense_grad_full[None]], 0)
    firsts_all = jnp.concatenate([expert_first_out, dense_first_full[None]], 0)
    bases_all = jnp.concatenate([expert_basis, dense_basis[None]], 0)
    seconds_all = jnp.concatenate([expert_second, dense_second[None]], 0)
    columns = grads_all.shape[2]
    rotated = jnp.einsum(
        "bki,bkc->bic", bases_all, jnp.concatenate([grads_all, firsts_all], 2), precision=HIGHEST
    )
    grad_rot = rotated[:, :, :columns]
    first_rot = rotated[:, :, columns:]
    seconds_out = 0.95 * seconds_all + 0.05 * grad_rot * grad_rot
    scaled = first_rot / (jnp.sqrt(seconds_out) + 1e-08)
    update = jnp.einsum("bik,bkc->bic", bases_all, scaled, precision=HIGHEST)
    expert_master_out = expert_master - 0.05 * update[:experts_here]
    dense_rows_here = dense_master.shape[0]
    dense_update = lax.dynamic_slice_in_dim(
        update[experts_here], lax.axis_index("wshard") * dense_rows_here, dense_rows_here, 0
    )
    dense_master_out = dense_master - 0.05 * dense_update
    expert_weights, dense_weights = (
        lax.all_gather(expert_master_out.astype(jnp.bfloat16), "dp", axis=2, tiled=True),
        lax.all_gather(dense_master_out.astype(jnp.bfloat16), "dp", axis=1, tiled=True),
    )
    partial_stat = jnp.concatenate(
        [
            jnp.einsum("bic,bjc->bij", expert_mean, expert_mean, precision=HIGHEST),
            jnp.einsum("ic,jc->ij", dense_grad_full, dense_grad_full, precision=HIGHEST)[None],
        ],
        0,
    )
    stats_all = jnp.concatenate([expert_stat, dense_stat[None]], 0)
    stat_rows = stats_all.shape[1]
    row_start = lax.axis_index(("tensor", "dp")) * stat_rows
    placed = lax.dynamic_update_slice_in_dim(
        jnp.zeros_like(partial_stat), 0.95 * stats_all, row_start, 1
    )
    stats_full = lax.psum(placed + 0.05 * partial_stat, ("tensor", "dp"))
    stats_full, expert_weights, dense_weights, expert_master_out, dense_master_out = (
        lax.optimization_barrier(
            (stats_full, expert_weights, dense_weights, expert_master_out, dense_master_out)
        )
    )
    stats_out = lax.dynamic_slice_in_dim(stats_full, row_start, stat_rows, 1)
    tensor_size = lax.axis_size("tensor")
    core = lax.axis_index("tensor") % 2
    stat_mine = lax.dynamic_slice_in_dim(stats_full, core, 1, 0)
    basis_mine = lax.dynamic_slice_in_dim(bases_all, core, 1, 0)
    power = jnp.einsum("bik,bkj->bij", stat_mine, basis_mine, precision=HIGH)
    square_sum = jnp.sum(power * power, (1, 2))
    current = power * lax.rsqrt(square_sum + 1e-06)[:, None, None]

    def ns_iteration(repeat, current):
        return quintic_step(current, local_gram(current))

    current = lax.fori_loop(0, NS_ITERS, ns_iteration, current)
    partner = lax.ppermute(
        current, "tensor", perm=[(t, t ^ 1) for t in range(tensor_size)]
    )
    expert_basis_out = jnp.where(core == 0, current, partner)
    dense_basis_out = jnp.where(core == 0, partner, current)[0]
    return (
        expert_master_out,
        expert_first_out,
        seconds_out[:experts_here],
        stats_out[:experts_here],
        expert_basis_out,
        expert_weights,
        dense_master_out,
        dense_first_out,
        seconds_out[experts_here],
        stats_out[experts_here],
        dense_basis_out,
        dense_weights,
    )


def solution(mesh):
    in_specs = (
        P("dp", "wshard", None, "tensor"),
        P("dp", "wshard", "tensor"),
        P("wshard", None, ("tensor", "dp")),
        P("wshard", None, ("tensor", "dp")),
        P("wshard", None, ("tensor", "dp")),
        P("wshard", ("tensor", "dp"), None),
        P("wshard", None, None),
        P("wshard", ("tensor", "dp")),
        P("wshard", ("tensor", "dp")),
        P(None, ("tensor", "dp")),
        P(("tensor", "dp"), None),
        P(),
    )
    out_specs = (
        P("wshard", None, ("tensor", "dp")),
        P("wshard", None, ("tensor", "dp")),
        P("wshard", None, ("tensor", "dp")),
        P("wshard", ("tensor", "dp"), None),
        P("wshard", None, None),
        P("wshard", None, "tensor"),
        P("wshard", ("tensor", "dp")),
        P("wshard", ("tensor", "dp")),
        P(None, ("tensor", "dp")),
        P(("tensor", "dp"), None),
        P(),
        P("wshard", "tensor"),
    )
    return jax.shard_map(shards, mesh=mesh, in_specs=in_specs, out_specs=out_specs, check_vma=False)
```

```python
import jax
import jax.numpy as jnp
from jax import lax
from jax.sharding import PartitionSpec as P

NS_ITERS = 3


HIGHEST = lax.Precision.HIGHEST
HIGH = lax.Precision.HIGH
linear_coef = 3.4445
cubic_coef = -4.775
quintic_coef = 2.0315


def local_gram(current):
    return jnp.einsum("bik,bjk->bij", current, current, precision=HIGH)


def quintic_step(current, gram_matrix):
    first_prod = jnp.einsum("bik,bkj->bij", gram_matrix, current, precision=HIGH)
    second_prod = jnp.einsum("bik,bkj->bij", gram_matrix, first_prod, precision=HIGH)
    return linear_coef * current + cubic_coef * first_prod + quintic_coef * second_prod


def replica_sum(local, axis):
    replicas = lax.axis_size(axis)
    here = lax.axis_index(axis)
    owned = local.shape[1] // replicas
    chunks = local.reshape(local.shape[0], replicas, owned).transpose(1, 0, 2)
    total = lax.dynamic_index_in_dim(chunks, here, 0, keepdims=False).astype(jnp.float32)
    for shift in range(1, replicas):
        outgoing = lax.dynamic_index_in_dim(chunks, (here + shift) % replicas, 0, keepdims=False)
        incoming = lax.ppermute(
            outgoing, axis, perm=[(i, (i + shift) % replicas) for i in range(replicas)]
        )
        total = total + incoming.astype(jnp.float32)
    return total


def gather_rows(block, axis):
    size = lax.axis_size(axis)
    here = lax.axis_index(axis)
    rows = block.shape[0]
    full = jnp.zeros((size * rows,) + block.shape[1:], block.dtype)
    full = lax.dynamic_update_slice_in_dim(full, block, here * rows, 0)
    for shift in range(1, size):
        moved = lax.ppermute(block, axis, perm=[(i, (i + shift) % size) for i in range(size)])
        source = (here - shift) % size
        full = lax.dynamic_update_slice_in_dim(full, moved, source * rows, 0)
    return full


def shards(
    expert_grads,
    dense_grads,
    expert_master,
    expert_first,
    expert_second,
    expert_stat,
    expert_basis,
    dense_master,
    dense_first,
    dense_second,
    dense_stat,
    dense_basis,
):
    replicas = lax.axis_size("dp")
    experts_here = expert_grads.shape[1]
    expert_local = expert_grads.reshape(expert_grads.shape[2:])
    dense_local = dense_grads.reshape(dense_grads.shape[1:])
    dense_sum = replica_sum(dense_local, "dp")
    expert_sum = replica_sum(expert_local, "dp")[None]
    expert_mean = expert_sum / replicas
    dense_mean = dense_sum / replicas
    expert_first_out = 0.9 * expert_first + 0.1 * expert_mean
    dense_first_out = 0.9 * dense_first + 0.1 * dense_mean
    dense_grad_full = gather_rows(dense_mean, "wshard")
    dense_first_full = lax.all_gather(dense_first_out, "wshard", axis=0, tiled=True)
    grads_all = jnp.concatenate([expert_mean, dense_grad_full[None]], 0)
    firsts_all = jnp.concatenate([expert_first_out, dense_first_full[None]], 0)
    bases_all = jnp.concatenate([expert_basis, dense_basis[None]], 0)
    seconds_all = jnp.concatenate([expert_second, dense_second[None]], 0)
    columns = grads_all.shape[2]
    rotated = jnp.einsum(
        "bki,bkc->bic", bases_all, jnp.concatenate([grads_all, firsts_all], 2), precision=HIGHEST
    )
    grad_rot = rotated[:, :, :columns]
    first_rot = rotated[:, :, columns:]
    seconds_out = 0.95 * seconds_all + 0.05 * grad_rot * grad_rot
    scaled = first_rot / (jnp.sqrt(seconds_out) + 1e-08)
    update = jnp.einsum("bik,bkc->bic", bases_all, scaled, precision=HIGHEST)
    expert_master_out = expert_master - 0.05 * update[:experts_here]
    dense_rows_here = dense_master.shape[0]
    dense_update = lax.dynamic_slice_in_dim(
        update[experts_here], lax.axis_index("wshard") * dense_rows_here, dense_rows_here, 0
    )
    dense_master_out = dense_master - 0.05 * dense_update
    expert_weights, dense_weights = (
        lax.all_gather(expert_master_out.astype(jnp.bfloat16), "dp", axis=2, tiled=True),
        lax.all_gather(dense_master_out.astype(jnp.bfloat16), "dp", axis=1, tiled=True),
    )
    partial_stat = jnp.concatenate(
        [
            jnp.einsum("bic,bjc->bij", expert_mean, expert_mean, precision=HIGHEST),
            jnp.einsum("ic,jc->ij", dense_grad_full, dense_grad_full, precision=HIGHEST)[None],
        ],
        0,
    )
    stats_all = jnp.concatenate([expert_stat, dense_stat[None]], 0)
    stat_rows = stats_all.shape[1]
    row_start = lax.axis_index(("tensor", "dp")) * stat_rows
    placed = lax.dynamic_update_slice_in_dim(
        jnp.zeros_like(partial_stat), 0.95 * stats_all, row_start, 1
    )
    stats_full = lax.psum(placed + 0.05 * partial_stat, ("tensor", "dp"))
    stats_full, expert_weights, dense_weights, expert_master_out, dense_master_out = (
        lax.optimization_barrier(
            (stats_full, expert_weights, dense_weights, expert_master_out, dense_master_out)
        )
    )
    stats_out = lax.dynamic_slice_in_dim(stats_full, row_start, stat_rows, 1)
    tensor_size = lax.axis_size("tensor")
    core = lax.axis_index("tensor") % 2
    stat_mine = lax.dynamic_slice_in_dim(stats_full, core, 1, 0)
    basis_mine = lax.dynamic_slice_in_dim(bases_all, core, 1, 0)
    power = jnp.einsum("bik,bkj->bij", stat_mine, basis_mine, precision=HIGH)
    square_sum = jnp.sum(power * power, (1, 2))
    current = power * lax.rsqrt(square_sum + 1e-06)[:, None, None]

    def ns_iteration(repeat, current):
        return quintic_step(current, local_gram(current))

    current = lax.fori_loop(0, NS_ITERS, ns_iteration, current)
    partner = lax.ppermute(
        current, "tensor", perm=[(t, t ^ 1) for t in range(tensor_size)]
    )
    expert_basis_out = jnp.where(core == 0, current, partner)
    dense_basis_out = jnp.where(core == 0, partner, current)[0]
    return (
        expert_master_out,
        expert_first_out,
        seconds_out[:experts_here],
        stats_out[:experts_here],
        expert_basis_out,
        expert_weights,
        dense_master_out,
        dense_first_out,
        seconds_out[experts_here],
        stats_out[experts_here],
        dense_basis_out,
        dense_weights,
    )


def solution(mesh):
    in_specs = (
        P("dp", "wshard", None, "tensor"),
        P("dp", "wshard", "tensor"),
        P("wshard", None, ("tensor", "dp")),
        P("wshard", None, ("tensor", "dp")),
        P("wshard", None, ("tensor", "dp")),
        P("wshard", ("tensor", "dp"), None),
        P("wshard", None, None),
        P("wshard", ("tensor", "dp")),
        P("wshard", ("tensor", "dp")),
        P(None, ("tensor", "dp")),
        P(("tensor", "dp"), None),
        P(),
    )
    out_specs = (
        P("wshard", None, ("tensor", "dp")),
        P("wshard", None, ("tensor", "dp")),
        P("wshard", None, ("tensor", "dp")),
        P("wshard", ("tensor", "dp"), None),
        P("wshard", None, None),
        P("wshard", None, "tensor"),
        P("wshard", ("tensor", "dp")),
        P("wshard", ("tensor", "dp")),
        P(None, ("tensor", "dp")),
        P(("tensor", "dp"), None),
        P(),
        P("wshard", "tensor"),
    )
    return jax.shard_map(shards, mesh=mesh, in_specs=in_specs, out_specs=out_specs, check_vma=False)
```

```python
import jax
import jax.numpy as jnp
from jax import lax
from jax.sharding import PartitionSpec as P

NS_ITERS = 3


HIGHEST = lax.Precision.HIGHEST
HIGH = lax.Precision.HIGH
linear_coef = 3.4445
cubic_coef = -4.775
quintic_coef = 2.0315


def local_gram(current):
    return jnp.einsum("bik,bjk->bij", current, current, precision=HIGH)


def quintic_step(current, gram_matrix):
    first_prod = jnp.einsum("bik,bkj->bij", gram_matrix, current, precision=HIGH)
    second_prod = jnp.einsum("bik,bkj->bij", gram_matrix, first_prod, precision=HIGH)
    return linear_coef * current + cubic_coef * first_prod + quintic_coef * second_prod


def gather_rows(block, axis):
    size = lax.axis_size(axis)
    here = lax.axis_index(axis)
    rows = block.shape[0]
    full = jnp.zeros((size * rows,) + block.shape[1:], block.dtype)
    full = lax.dynamic_update_slice_in_dim(full, block, here * rows, 0)
    for shift in range(1, size):
        moved = lax.ppermute(block, axis, perm=[(i, (i + shift) % size) for i in range(size)])
        source = (here - shift) % size
        full = lax.dynamic_update_slice_in_dim(full, moved, source * rows, 0)
    return full


def shards(
    expert_grads,
    dense_grads,
    expert_master,
    expert_first,
    expert_second,
    expert_stat,
    expert_basis,
    dense_master,
    dense_first,
    dense_second,
    dense_stat,
    dense_basis,
):
    replicas = lax.axis_size("dp")
    experts_here = expert_grads.shape[1]
    expert_local = expert_grads.reshape(expert_grads.shape[2:])
    dense_local = dense_grads.reshape(dense_grads.shape[1:])
    expert_rows = expert_local.shape[0]
    joined = jnp.concatenate([expert_local, dense_local], 0)
    owned = joined.shape[1] // replicas
    joined = joined.reshape(joined.shape[0], replicas, owned)
    received = lax.all_to_all(joined, "dp", 1, 1, tiled=True)
    joined_sum = jnp.sum(received.astype(jnp.float32), 1)
    expert_sum = joined_sum[None, :expert_rows]
    dense_sum = joined_sum[expert_rows:]
    expert_mean = expert_sum / replicas
    dense_mean = dense_sum / replicas
    expert_first_out = 0.9 * expert_first + 0.1 * expert_mean
    dense_first_out = 0.9 * dense_first + 0.1 * dense_mean
    dense_grad_full = gather_rows(dense_mean, "wshard")
    dense_first_full = lax.all_gather(dense_first_out, "wshard", axis=0, tiled=True)
    grads_all = jnp.concatenate([expert_mean, dense_grad_full[None]], 0)
    firsts_all = jnp.concatenate([expert_first_out, dense_first_full[None]], 0)
    bases_all = jnp.concatenate([expert_basis, dense_basis[None]], 0)
    seconds_all = jnp.concatenate([expert_second, dense_second[None]], 0)
    columns = grads_all.shape[2]
    rotated = jnp.einsum(
        "bki,bkc->bic", bases_all, jnp.concatenate([grads_all, firsts_all], 2), precision=HIGHEST
    )
    grad_rot = rotated[:, :, :columns]
    first_rot = rotated[:, :, columns:]
    seconds_out = 0.95 * seconds_all + 0.05 * grad_rot * grad_rot
    scaled = first_rot / (jnp.sqrt(seconds_out) + 1e-08)
    update = jnp.einsum("bik,bkc->bic", bases_all, scaled, precision=HIGHEST)
    expert_master_out = expert_master - 0.05 * update[:experts_here]
    dense_rows_here = dense_master.shape[0]
    dense_update = lax.dynamic_slice_in_dim(
        update[experts_here], lax.axis_index("wshard") * dense_rows_here, dense_rows_here, 0
    )
    dense_master_out = dense_master - 0.05 * dense_update
    expert_weights, dense_weights = (
        lax.all_gather(expert_master_out.astype(jnp.bfloat16), "dp", axis=2, tiled=True),
        lax.all_gather(dense_master_out.astype(jnp.bfloat16), "dp", axis=1, tiled=True),
    )
    partial_stat = jnp.concatenate(
        [
            jnp.einsum("bic,bjc->bij", expert_mean, expert_mean, precision=HIGHEST),
            jnp.einsum("ic,jc->ij", dense_grad_full, dense_grad_full, precision=HIGHEST)[None],
        ],
        0,
    )
    stats_all = jnp.concatenate([expert_stat, dense_stat[None]], 0)
    stat_rows = stats_all.shape[1]
    row_start = lax.axis_index(("tensor", "dp")) * stat_rows
    placed = lax.dynamic_update_slice_in_dim(
        jnp.zeros_like(partial_stat), 0.95 * stats_all, row_start, 1
    )
    stats_full = lax.psum(placed + 0.05 * partial_stat, ("tensor", "dp"))
    stats_full, expert_weights, dense_weights, expert_master_out, dense_master_out = (
        lax.optimization_barrier(
            (stats_full, expert_weights, dense_weights, expert_master_out, dense_master_out)
        )
    )
    stats_out = lax.dynamic_slice_in_dim(stats_full, row_start, stat_rows, 1)
    tensor_size = lax.axis_size("tensor")
    core = lax.axis_index("tensor") % 2
    stat_mine = lax.dynamic_slice_in_dim(stats_full, core, 1, 0)
    basis_mine = lax.dynamic_slice_in_dim(bases_all, core, 1, 0)
    power = jnp.einsum("bik,bkj->bij", stat_mine, basis_mine, precision=HIGH)
    square_sum = jnp.sum(power * power, (1, 2))
    current = power * lax.rsqrt(square_sum + 1e-06)[:, None, None]

    def ns_iteration(repeat, current):
        return quintic_step(current, local_gram(current))

    current = lax.fori_loop(0, NS_ITERS, ns_iteration, current)
    partner = lax.ppermute(
        current, "tensor", perm=[(t, t ^ 1) for t in range(tensor_size)]
    )
    expert_basis_out = jnp.where(core == 0, current, partner)
    dense_basis_out = jnp.where(core == 0, partner, current)[0]
    return (
        expert_master_out,
        expert_first_out,
        seconds_out[:experts_here],
        stats_out[:experts_here],
        expert_basis_out,
        expert_weights,
        dense_master_out,
        dense_first_out,
        seconds_out[experts_here],
        stats_out[experts_here],
        dense_basis_out,
        dense_weights,
    )


def solution(mesh):
    in_specs = (
        P("dp", "wshard", None, "tensor"),
        P("dp", "wshard", "tensor"),
        P("wshard", None, ("tensor", "dp")),
        P("wshard", None, ("tensor", "dp")),
        P("wshard", None, ("tensor", "dp")),
        P("wshard", ("tensor", "dp"), None),
        P("wshard", None, None),
        P("wshard", ("tensor", "dp")),
        P("wshard", ("tensor", "dp")),
        P(None, ("tensor", "dp")),
        P(("tensor", "dp"), None),
        P(),
    )
    out_specs = (
        P("wshard", None, ("tensor", "dp")),
        P("wshard", None, ("tensor", "dp")),
        P("wshard", None, ("tensor", "dp")),
        P("wshard", ("tensor", "dp"), None),
        P("wshard", None, None),
        P("wshard", None, "tensor"),
        P("wshard", ("tensor", "dp")),
        P("wshard", ("tensor", "dp")),
        P(None, ("tensor", "dp")),
        P(("tensor", "dp"), None),
        P(),
        P("wshard", "tensor"),
    )
    return jax.shard_map(shards, mesh=mesh, in_specs=in_specs, out_specs=out_specs, check_vma=False)
```
